512 devices in a mesh: band: 32 (over y, x, z_hi), slab: 16 (over z_lo, core).
Axes of the slice: x: 4, y: 4, z: 16 (z_hi: 2, z_lo: 8; z = z_hi * 8 + z_lo), core: 2. Of those that a mesh axis runs over, the one named last changes fastest.
Arguments:
- wave_coeffs: float32 [64, 2, 128, 128, 128], P('band', None, 'slab'), may hold values from -12 to 12
- column_mask: int32 [128, 128], replicated, may hold values from 0 to 1, as said below
- occupations: float32 [64], P('band'), may hold values from 0.1 to 2
- core_density: float32 [128, 128, 128], P('band', 'slab'), may hold values from 0.05 to 0.5
Outputs:
- hartree: float32 [128, 128, 128], P('band', 'slab')
- xc_potential: float32 [128, 128, 128], P('band', 'slab')
The draws below stay inside these ranges and needn't reach their ends.
Inputs may be any that keep to these rules, and one draw needn't show every extreme that they name: `column_mask`: 1 marks a column of frequencies (first two indices) inside the cutoff; only columns whose shifted indices s1, s2 satisfy s1^2 + s2^2 <= 32^2 can be 1.
All inputs are finite; a program needn't handle non-finite values.
Results may differ from the reference program's by a relative error of at most 0.00035.
Values sent between devices are 32-bit elements; how exact they have to be, the bound alone decides.
No kernel may reach another device: no remote copies, remote signals or barrier semaphores. Data moves between devices by JAX's collectives and lax.ppermute only.
A program may use at most 64 MiB of HBM per device.

```python
import math
import jax
import jax.numpy as jnp
from jax import lax

N = 128
BANDS = 64


def draw_column_mask(key, part):
    indices = jnp.arange(N, dtype=jnp.int32)
    shifted = (indices + N // 2) % N - N // 2
    squared = shifted[:, None] * shifted[:, None] + shifted[None, :] * shifted[None, :]
    radius = N // 4
    inside = squared <= radius * radius
    keeper = jax.random.randint(jax.random.fold_in(key, 17), (N, N), 0, 8) != 0
    return jnp.where(inside & keeper, 1, 0).astype(jnp.int32)


def shard_levels(rng, shape, shards, least, largest):
    loudness, own = 1.0, jax.random.fold_in(rng, 6)
    for dim, parts in shards:
        draws = jnp.exp(jax.random.uniform(jax.random.fold_in(own, dim), (parts,), jnp.float32, least / len(shards), largest / len(shards)))
        loudness = loudness * jnp.repeat(draws, shape[dim] // parts).reshape([-1 if axis == dim else 1 for axis in range(len(shape))])
    return loudness


def centred(own_key, dims, scale, most, cuts=(), kind=jnp.bfloat16):
    factor_of = shard_levels(own_key, dims, cuts, -0.22, 0.18) if cuts else 1.0
    values = jax.random.normal(own_key, dims, jnp.float32) * scale * factor_of
    return jnp.minimum(jnp.maximum(values, -most), most).astype(kind)


def setup_inputs(seed: int = 0) -> dict:
    arg_keys = jax.random.split(jax.random.key(seed), 5)
    wave_coeffs = centred(arg_keys[0], (BANDS, 2, N, N, N), 2.0, 12.0, ((0, 32), (2, 16)), jnp.float32)
    column_mask = draw_column_mask(jax.random.fold_in(arg_keys[4], 71), 0)
    occupations = jnp.clip(jnp.exp(math.log(2.0) - 2.9957323 * jax.random.uniform(arg_keys[2], (BANDS,), jnp.float32) ** shard_levels(arg_keys[2], (BANDS,), ((0, 32),), -0.2, 0.2)), 0.1, 2.0)
    core_density = jnp.clip(jnp.exp(math.log(0.5) - 2.3025851 * jax.random.uniform(arg_keys[3], (N, N, N), jnp.float32) ** shard_levels(arg_keys[3], (N, N, N), ((0, 32), (1, 16)), -0.2, 0.2)), 0.05, 0.5)
    return {"wave_coeffs": wave_coeffs, "column_mask": column_mask, "occupations": occupations, "core_density": core_density}


grid_spacing = 0.59
wigner_a = 0.44
wigner_b = 7.8


def kernel_block(extent, starts, amounts):
    pieces = []
    for offset, amount in zip(starts, amounts):
        frequency = offset + jnp.arange(amount, dtype=jnp.int32)
        shifted = (frequency + extent // 2) % extent - extent // 2
        pieces.append(shifted * shifted)
    squared = pieces[0][:, None, None] + pieces[1][None, :, None] + pieces[2][None, None, :]
    length = extent * grid_spacing
    scaled = (length * length / math.pi) / jnp.maximum(squared, 1).astype(jnp.float32)
    return jnp.where(squared == 0, 0.0, scaled)


def exchange_correlation(density):
    root_density = jnp.cbrt(density)
    radius = (3.0 / (4.0 * math.pi)) ** (1.0 / 3.0) / root_density
    exchange_part = -((3.0 / math.pi) ** (1.0 / 3.0)) * root_density
    shifted = radius + wigner_b
    correlation = -wigner_a / shifted - wigner_a * radius / (3.0 * shifted * shifted)
    return exchange_part + correlation


def reference(wave_coeffs, column_mask, occupations, core_density):
    inside = column_mask.astype(jnp.float32)[:, :, None]
    factor = float(N) ** 1.5

    def add_band(running, entries):
        coefficient, weight = entries
        wavefunction = jnp.fft.ifftn((coefficient[0] + 1j * coefficient[1]) * inside) * factor
        modulus = wavefunction.real * wavefunction.real + wavefunction.imag * wavefunction.imag
        return running + weight * modulus, None

    summed, _ = lax.scan(add_band, jnp.zeros((N, N, N), jnp.float32), (wave_coeffs, occupations))
    valence = summed / BANDS
    spectrum = jnp.fft.fftn(valence)
    hartree = jnp.fft.ifftn(spectrum * kernel_block(N, (0, 0, 0), (N, N, N))).real
    xc_potential = exchange_correlation(valence + core_density)
    return hartree, xc_potential
```

```python
import math

import jax
import jax.numpy as jnp
from jax import lax
from jax.sharding import PartitionSpec as P

grid_spacing = 0.59
wigner_a = 0.44
wigner_b = 7.8


def dft_tables(extent):
    indices = jnp.arange(extent, dtype=jnp.int32)
    phase = indices[:, None] * indices[None, :] % extent
    angle = phase.astype(jnp.float32) * (2.0 * math.pi / extent)
    return (jnp.cos(angle), jnp.sin(angle))


def kernel_block(extent, starts, amounts):
    pieces = []
    for offset, amount in zip(starts, amounts):
        frequency = offset + jnp.arange(amount, dtype=jnp.int32)
        shifted = (frequency + extent // 2) % extent - extent // 2
        pieces.append(shifted * shifted)
    squared = pieces[0][:, None, None] + pieces[1][None, :, None] + pieces[2][None, None, :]
    length = extent * grid_spacing
    scaled = length * length / math.pi / jnp.maximum(squared, 1).astype(jnp.float32)
    return jnp.where(squared == 0, 0.0, scaled)


def exchange_correlation(density):
    root_density = jnp.cbrt(density)
    radius = (3.0 / (4.0 * math.pi)) ** (1.0 / 3.0) / root_density
    exchange_part = -((3.0 / math.pi) ** (1.0 / 3.0)) * root_density
    shifted = radius + wigner_b
    correlation = -wigner_a / shifted - wigner_a * radius / (3.0 * shifted * shifted)
    return exchange_part + correlation


def project(pattern, values, matrix):
    return jnp.einsum(pattern, values, matrix, precision=lax.Precision.HIGHEST)


def rotate(real_part, imag_part, pattern, cosine_table, sine_table, direction):
    new_real = project(pattern, real_part, cosine_table) - direction * project(
        pattern, imag_part, sine_table
    )
    new_imag = direction * project(pattern, real_part, sine_table) + project(
        pattern, imag_part, cosine_table
    )
    return (new_real, new_imag)


def local(wave_coeffs, column_mask, occupations, core_density):
    local_bands = wave_coeffs.shape[0]
    row_count = wave_coeffs.shape[2]
    extent = wave_coeffs.shape[3]
    bands_all = lax.axis_size("band") * local_bands
    band_rows = extent // lax.axis_size("band")
    slab_index = lax.axis_index("slab")
    band_index = lax.axis_index("band")
    cosine_table, sine_table = dft_tables(extent)
    mask_rows = lax.dynamic_slice_in_dim(column_mask, slab_index * row_count, row_count, 0).astype(
        jnp.float32
    )
    masked = wave_coeffs * mask_rows[None, None, :, :, None]
    real_part, imag_part = rotate(
        masked[:, 0], masked[:, 1], "bxyz,zw->bxyw", cosine_table, sine_table, 1.0
    )
    real_part, imag_part = rotate(
        real_part, imag_part, "bxyz,yw->bxwz", cosine_table, sine_table, 1.0
    )
    stacked = jnp.stack((real_part, imag_part), axis=1)
    factor = 1.0 / (float(extent) ** 3 * bands_all)
    partial_value = jnp.zeros((extent, row_count, extent), jnp.float32)
    for member in range(local_bands):
        arrived = lax.all_to_all(stacked[member], "slab", split_axis=2, concat_axis=1, tiled=True)
        plane_real, plane_imag = rotate(
            arrived[0], arrived[1], "xyz,xw->wyz", cosine_table, sine_table, 1.0
        )
        partial_value = partial_value + occupations[member] * (
            plane_real * plane_real + plane_imag * plane_imag
        )
    partial_value = partial_value * factor
    first_real = project("xyz,zw->xyw", partial_value, cosine_table)
    first_imag = -project("xyz,zw->xyw", partial_value, sine_table)
    line_real, line_imag = rotate(
        first_real, first_imag, "xyz,xw->wyz", cosine_table, sine_table, -1.0
    )
    arrived = lax.all_to_all(
        jnp.stack((line_real, line_imag)), "slab", split_axis=1, concat_axis=2, tiled=True
    )
    line_real, line_imag = rotate(
        arrived[0], arrived[1], "xyz,yw->xwz", cosine_table, sine_table, -1.0
    )
    kernel = kernel_block(extent, (slab_index * row_count, 0, 0), (row_count, extent, extent))
    line_real, line_imag = rotate(
        kernel * line_real, kernel * line_imag, "xyz,yw->xwz", cosine_table, sine_table, 1.0
    )
    arrived = lax.all_to_all(
        jnp.stack((line_real, line_imag)), "slab", split_axis=2, concat_axis=1, tiled=True
    )
    line_real, line_imag = rotate(
        arrived[0], arrived[1], "xyz,xw->wyz", cosine_table, sine_table, 1.0
    )
    spatial = project("xyz,zw->xyw", line_real, cosine_table) - project(
        "xyz,zw->xyw", line_imag, sine_table
    )
    partial_hartree = spatial / float(extent) ** 3
    band_count = lax.axis_size("band")
    both = jnp.stack((partial_value, partial_hartree)).reshape(
        2, band_count, band_rows, row_count, extent
    )
    summed = lax.all_to_all(both, "band", split_axis=1, concat_axis=1, tiled=True).sum(axis=1)
    own_density, hartree = summed[0], summed[1]
    xc_potential = exchange_correlation(own_density + core_density)
    return (hartree, xc_potential)


def solution(mesh):
    return jax.shard_map(
        local,
        mesh=mesh,
        in_specs=(P("band", None, "slab", None, None), P(), P("band"), P("band", "slab", None)),
        out_specs=(P("band", "slab", None), P("band", "slab", None)),
        check_vma=False,
    )
```

```python
import math

import jax
import jax.numpy as jnp
from jax import lax
from jax.sharding import PartitionSpec as P

grid_spacing = 0.59
wigner_a = 0.44
wigner_b = 7.8


def dft_tables(extent):
    indices = jnp.arange(extent, dtype=jnp.int32)
    phase = indices[:, None] * indices[None, :] % extent
    angle = phase.astype(jnp.float32) * (2.0 * math.pi / extent)
    return (jnp.cos(angle), jnp.sin(angle))


def kernel_block(extent, starts, amounts):
    pieces = []
    for offset, amount in zip(starts, amounts):
        frequency = offset + jnp.arange(amount, dtype=jnp.int32)
        shifted = (frequency + extent // 2) % extent - extent // 2
        pieces.append(shifted * shifted)
    squared = pieces[0][:, None, None] + pieces[1][None, :, None] + pieces[2][None, None, :]
    length = extent * grid_spacing
    scaled = length * length / math.pi / jnp.maximum(squared, 1).astype(jnp.float32)
    return jnp.where(squared == 0, 0.0, scaled)


def exchange_correlation(density):
    root_density = jnp.cbrt(density)
    radius = (3.0 / (4.0 * math.pi)) ** (1.0 / 3.0) / root_density
    exchange_part = -((3.0 / math.pi) ** (1.0 / 3.0)) * root_density
    shifted = radius + wigner_b
    correlation = -wigner_a / shifted - wigner_a * radius / (3.0 * shifted * shifted)
    return exchange_part + correlation


def project(pattern, values, matrix):
    return jnp.einsum(pattern, values, matrix, precision=lax.Precision.HIGHEST)


def rotate(real_part, imag_part, pattern, cosine_table, sine_table, direction):
    new_real = project(pattern, real_part, cosine_table) - direction * project(
        pattern, imag_part, sine_table
    )
    new_imag = direction * project(pattern, real_part, sine_table) + project(
        pattern, imag_part, cosine_table
    )
    return (new_real, new_imag)


def real_basis(extent):
    half = extent // 2
    indices = jnp.arange(extent, dtype=jnp.int32)
    frequency = jnp.where(indices <= half, indices, indices - half)
    phase = frequency[:, None] * indices[None, :] % extent
    angle = phase.astype(jnp.float32) * (2.0 * math.pi / extent)
    basis = jnp.where((indices <= half)[:, None], jnp.cos(angle), jnp.sin(angle))
    weight = jnp.where((indices == 0) | (indices == half), 1.0, 2.0).astype(jnp.float32)
    return basis, frequency, weight


def real_kernel_block(extent, frequency, weight, start, amount):
    rows = lax.dynamic_slice_in_dim(frequency, start, amount, 0)
    row_weight = lax.dynamic_slice_in_dim(weight, start, amount, 0)
    squared = (
        (rows * rows)[:, None, None]
        + (frequency * frequency)[None, :, None]
        + (frequency * frequency)[None, None, :]
    )
    length = extent * grid_spacing
    scaled = length * length / math.pi / jnp.maximum(squared, 1).astype(jnp.float32)
    kernel = jnp.where(squared == 0, 0.0, scaled)
    scale = row_weight[:, None, None] * weight[None, :, None] * weight[None, None, :]
    return kernel * scale / float(extent) ** 3


def local(wave_coeffs, column_mask, occupations, core_density):
    local_bands = wave_coeffs.shape[0]
    row_count = wave_coeffs.shape[2]
    extent = wave_coeffs.shape[3]
    band_count = lax.axis_size("band")
    bands_all = band_count * local_bands
    band_rows = extent // band_count
    slab_index = lax.axis_index("slab")
    cosine_table, sine_table = dft_tables(extent)
    mask_rows = lax.dynamic_slice_in_dim(column_mask, slab_index * row_count, row_count, 0).astype(
        jnp.float32
    )
    masked = wave_coeffs * mask_rows[None, None, :, :, None]
    real_part, imag_part = rotate(
        masked[:, 0], masked[:, 1], "bxyz,zw->bxyw", cosine_table, sine_table, 1.0
    )
    real_part, imag_part = rotate(
        real_part, imag_part, "bxyz,yw->bxwz", cosine_table, sine_table, 1.0
    )
    stacked = jnp.stack((real_part, imag_part), axis=1)
    arrived = lax.all_to_all(stacked, "slab", split_axis=3, concat_axis=2, tiled=True)
    plane_real, plane_imag = rotate(
        arrived[:, 0], arrived[:, 1], "bxyz,xw->bwyz", cosine_table, sine_table, 1.0
    )
    factor = 1.0 / (float(extent) ** 3 * bands_all)
    weights = occupations * factor
    partial_value = jnp.einsum(
        "b,bxyz->xyz",
        weights,
        plane_real * plane_real + plane_imag * plane_imag,
        precision=lax.Precision.HIGHEST,
    )
    basis, frequency, weight = real_basis(extent)
    spectrum = project("xyz,mz->xym", partial_value, basis)
    spectrum = project("xyz,mx->myz", spectrum, basis)
    arrived = lax.all_to_all(spectrum, "slab", split_axis=0, concat_axis=1, tiled=True)
    spectrum = project("xyz,my->xmz", arrived, basis)
    kernel = real_kernel_block(extent, frequency, weight, slab_index * row_count, row_count)
    potential = project("xmz,my->xyz", kernel * spectrum, basis)
    arrived = lax.all_to_all(potential, "slab", split_axis=1, concat_axis=0, tiled=True)
    potential = project("myz,mx->xyz", arrived, basis)
    partial_hartree = project("xym,mz->xyz", potential, basis)
    both = jnp.stack((partial_value, partial_hartree)).reshape(
        2, band_count, band_rows, row_count, extent
    )
    summed = lax.all_to_all(both, "band", split_axis=1, concat_axis=1, tiled=True).sum(axis=1)
    own_density, hartree = summed[0], summed[1]
    xc_potential = exchange_correlation(own_density + core_density)
    return (hartree, xc_potential)


def solution(mesh):
    return jax.shard_map(
        local,
        mesh=mesh,
        in_specs=(P("band", None, "slab", None, None), P(), P("band"), P("band", "slab", None)),
        out_specs=(P("band", "slab", None), P("band", "slab", None)),
        check_vma=False,
    )
```

```python
import math

import jax
import jax.numpy as jnp
from jax import lax
from jax.sharding import PartitionSpec as P

grid_spacing = 0.59
wigner_a = 0.44
wigner_b = 7.8


def dft_tables(extent):
    indices = jnp.arange(extent, dtype=jnp.int32)
    phase = indices[:, None] * indices[None, :] % extent
    angle = phase.astype(jnp.float32) * (2.0 * math.pi / extent)
    return (jnp.cos(angle), jnp.sin(angle))


def kernel_block(extent, starts, amounts):
    pieces = []
    for offset, amount in zip(starts, amounts):
        frequency = offset + jnp.arange(amount, dtype=jnp.int32)
        shifted = (frequency + extent // 2) % extent - extent // 2
        pieces.append(shifted * shifted)
    squared = pieces[0][:, None, None] + pieces[1][None, :, None] + pieces[2][None, None, :]
    length = extent * grid_spacing
    scaled = length * length / math.pi / jnp.maximum(squared, 1).astype(jnp.float32)
    return jnp.where(squared == 0, 0.0, scaled)


def exchange_correlation(density):
    root_density = jnp.cbrt(density)
    radius = (3.0 / (4.0 * math.pi)) ** (1.0 / 3.0) / root_density
    exchange_part = -((3.0 / math.pi) ** (1.0 / 3.0)) * root_density
    shifted = radius + wigner_b
    correlation = -wigner_a / shifted - wigner_a * radius / (3.0 * shifted * shifted)
    return exchange_part + correlation


def project(pattern, values, matrix):
    return jnp.einsum(pattern, values, matrix, precision=lax.Precision.HIGHEST)


def rotate(real_part, imag_part, pattern, cosine_table, sine_table, direction):
    new_real = project(pattern, real_part, cosine_table) - direction * project(
        pattern, imag_part, sine_table
    )
    new_imag = direction * project(pattern, real_part, sine_table) + project(
        pattern, imag_part, cosine_table
    )
    return (new_real, new_imag)


def real_basis(extent):
    half = extent // 2
    indices = jnp.arange(extent, dtype=jnp.int32)
    frequency = jnp.where(indices <= half, indices, indices - half)
    phase = frequency[:, None] * indices[None, :] % extent
    angle = phase.astype(jnp.float32) * (2.0 * math.pi / extent)
    basis = jnp.where((indices <= half)[:, None], jnp.cos(angle), jnp.sin(angle))
    weight = jnp.where((indices == 0) | (indices == half), 1.0, 2.0).astype(jnp.float32)
    return basis, frequency, weight


def real_kernel_block(extent, frequency, weight, start, amount):
    rows = lax.dynamic_slice_in_dim(frequency, start, amount, 0)
    row_weight = lax.dynamic_slice_in_dim(weight, start, amount, 0)
    squared = (
        (rows * rows)[:, None, None]
        + (frequency * frequency)[None, :, None]
        + (frequency * frequency)[None, None, :]
    )
    length = extent * grid_spacing
    scaled = length * length / math.pi / jnp.maximum(squared, 1).astype(jnp.float32)
    kernel = jnp.where(squared == 0, 0.0, scaled)
    scale = row_weight[:, None, None] * weight[None, :, None] * weight[None, None, :]
    return kernel * scale / float(extent) ** 3


def support(values, axis, half_width):
    extent = values.shape[axis]
    low = lax.slice_in_dim(values, 0, half_width, axis=axis)
    high = lax.slice_in_dim(values, extent - half_width, extent, axis=axis)
    return jnp.concatenate((low, high), axis=axis)


def local(wave_coeffs, column_mask, occupations, core_density):
    local_bands = wave_coeffs.shape[0]
    row_count = wave_coeffs.shape[2]
    extent = wave_coeffs.shape[3]
    band_count = lax.axis_size("band")
    bands_all = band_count * local_bands
    band_rows = extent // band_count
    slab_index = lax.axis_index("slab")
    half_width = -(-(extent // 4 + 1) // 4) * 4
    cosine_table, sine_table = dft_tables(extent)
    cosine_kept = support(cosine_table, 0, half_width)
    sine_kept = support(sine_table, 0, half_width)
    mask_rows = lax.dynamic_slice_in_dim(column_mask, slab_index * row_count, row_count, 0)
    mask_kept = support(mask_rows, 1, half_width).astype(jnp.float32)
    masked = support(wave_coeffs, 3, half_width) * mask_kept[None, None, :, :, None]
    real_part, imag_part = rotate(
        masked[:, 0], masked[:, 1], "bxyz,zw->bwxy", cosine_table, sine_table, 1.0
    )
    stacked = jnp.stack((real_part, imag_part), axis=1)
    arrived = lax.all_to_all(stacked, "slab", split_axis=2, concat_axis=3, tiled=True)
    arrived = support(arrived, 3, half_width)
    real_part, imag_part = rotate(
        arrived[:, 0], arrived[:, 1], "bzxy,xw->bzwy", cosine_kept, sine_kept, 1.0
    )
    plane_real, plane_imag = rotate(
        real_part, imag_part, "bzxy,yw->bzxw", cosine_kept, sine_kept, 1.0
    )
    factor = 1.0 / (float(extent) ** 3 * bands_all)
    weights = occupations * factor
    partial_value = jnp.einsum(
        "b,bzxy->zxy",
        weights,
        plane_real * plane_real + plane_imag * plane_imag,
        precision=lax.Precision.HIGHEST,
    )
    basis, frequency, weight = real_basis(extent)
    spectrum = project("zxy,mx->zmy", partial_value, basis)
    spectrum = project("zxy,my->zxm", spectrum, basis)
    arrived = lax.all_to_all(spectrum, "slab", split_axis=1, concat_axis=0, tiled=True)
    spectrum = project("zxy,mz->mxy", arrived, basis)
    kernel = real_kernel_block(extent, frequency, weight, slab_index * row_count, row_count)
    kernel = jnp.transpose(kernel, (2, 0, 1))
    potential = project("mxy,mz->zxy", kernel * spectrum, basis)
    arrived = lax.all_to_all(potential, "slab", split_axis=0, concat_axis=1, tiled=True)
    potential = project("zmy,mx->zxy", arrived, basis)
    partial_hartree = project("zxm,my->zxy", potential, basis)
    both = jnp.stack((partial_value, partial_hartree)).reshape(
        2, row_count, band_count, band_rows, extent
    )
    summed = lax.all_to_all(both, "band", split_axis=2, concat_axis=2, tiled=True).sum(axis=2)
    placed = lax.all_to_all(summed, "slab", split_axis=3, concat_axis=1, tiled=True)
    placed = jnp.transpose(placed, (0, 2, 3, 1))
    own_density, hartree = placed[0], placed[1]
    xc_potential = exchange_correlation(own_density + core_density)
    return (hartree, xc_potential)


def solution(mesh):
    return jax.shard_map(
        local,
        mesh=mesh,
        in_specs=(P("band", None, "slab", None, None), P(), P("band"), P("band", "slab", None)),
        out_specs=(P("band", "slab", None), P("band", "slab", None)),
        check_vma=False,
    )
```

```python
import math

import jax
import jax.numpy as jnp
from jax import lax
from jax.sharding import Mesh, PartitionSpec as P

grid_spacing = 0.59
wigner_a = 0.44
wigner_b = 7.8


def dft_tables(extent):
    indices = jnp.arange(extent, dtype=jnp.int32)
    phase = indices[:, None] * indices[None, :] % extent
    angle = phase.astype(jnp.float32) * (2.0 * math.pi / extent)
    return (jnp.cos(angle), jnp.sin(angle))


def kernel_block(extent, starts, amounts):
    pieces = []
    for offset, amount in zip(starts, amounts):
        frequency = offset + jnp.arange(amount, dtype=jnp.int32)
        shifted = (frequency + extent // 2) % extent - extent // 2
        pieces.append(shifted * shifted)
    squared = pieces[0][:, None, None] + pieces[1][None, :, None] + pieces[2][None, None, :]
    length = extent * grid_spacing
    scaled = length * length / math.pi / jnp.maximum(squared, 1).astype(jnp.float32)
    return jnp.where(squared == 0, 0.0, scaled)


def exchange_correlation(density):
    root_density = jnp.cbrt(density)
    radius = (3.0 / (4.0 * math.pi)) ** (1.0 / 3.0) / root_density
    exchange_part = -((3.0 / math.pi) ** (1.0 / 3.0)) * root_density
    shifted = radius + wigner_b
    correlation = -wigner_a / shifted - wigner_a * radius / (3.0 * shifted * shifted)
    return exchange_part + correlation


def project(pattern, values, matrix):
    return jnp.einsum(pattern, values, matrix, precision=lax.Precision.HIGHEST)


def rotate(real_part, imag_part, pattern, cosine_table, sine_table, direction):
    new_real = project(pattern, real_part, cosine_table) - direction * project(
        pattern, imag_part, sine_table
    )
    new_imag = direction * project(pattern, real_part, sine_table) + project(
        pattern, imag_part, cosine_table
    )
    return (new_real, new_imag)


def real_basis(extent):
    half = extent // 2
    indices = jnp.arange(extent, dtype=jnp.int32)
    frequency = jnp.where(indices <= half, indices, indices - half)
    phase = frequency[:, None] * indices[None, :] % extent
    angle = phase.astype(jnp.float32) * (2.0 * math.pi / extent)
    basis = jnp.where((indices <= half)[:, None], jnp.cos(angle), jnp.sin(angle))
    weight = jnp.where((indices == 0) | (indices == half), 1.0, 2.0).astype(jnp.float32)
    return basis, frequency, weight


def real_kernel_block(extent, frequency, weight, start, amount):
    rows = lax.dynamic_slice_in_dim(frequency, start, amount, 0)
    row_weight = lax.dynamic_slice_in_dim(weight, start, amount, 0)
    squared = (
        (rows * rows)[:, None, None]
        + (frequency * frequency)[None, :, None]
        + (frequency * frequency)[None, None, :]
    )
    length = extent * grid_spacing
    scaled = length * length / math.pi / jnp.maximum(squared, 1).astype(jnp.float32)
    kernel = jnp.where(squared == 0, 0.0, scaled)
    scale = row_weight[:, None, None] * weight[None, :, None] * weight[None, None, :]
    return kernel * scale / float(extent) ** 3


def support(values, axis, half_width):
    extent = values.shape[axis]
    low = lax.slice_in_dim(values, 0, half_width, axis=axis)
    high = lax.slice_in_dim(values, extent - half_width, extent, axis=axis)
    return jnp.concatenate((low, high), axis=axis)


def local(wave_coeffs, column_mask, occupations, core_density):
    local_bands = wave_coeffs.shape[0]
    row_count = wave_coeffs.shape[2]
    extent = wave_coeffs.shape[3]
    plane_count = lax.axis_size("plane")
    half_count = lax.axis_size("half")
    band_count = plane_count * half_count
    bands_all = band_count * local_bands
    band_rows = extent // band_count
    slab_count = lax.axis_size("slab")
    slab_index = lax.axis_index("slab")
    half_width = -(-(extent // 4 + 1) // 4) * 4
    cosine_table, sine_table = dft_tables(extent)
    cosine_kept = support(cosine_table, 0, half_width)
    sine_kept = support(sine_table, 0, half_width)
    mask_rows = lax.dynamic_slice_in_dim(column_mask, slab_index * row_count, row_count, 0)
    mask_kept = support(mask_rows, 1, half_width).astype(jnp.float32)
    masked = support(wave_coeffs, 3, half_width) * mask_kept[None, None, :, :, None]
    real_part, imag_part = rotate(
        masked[:, 0], masked[:, 1], "bxyz,zw->wbxy", cosine_table, sine_table, 1.0
    )
    stacked = jnp.stack((real_part, imag_part), axis=2).reshape(
        slab_count, extent // slab_count, -1
    )
    arrived = lax.all_to_all(stacked, "slab", split_axis=0, concat_axis=0, tiled=True)
    arrived = arrived.reshape(
        slab_count, extent // slab_count, local_bands, 2, row_count, 2 * half_width
    )
    blocked_cosine = cosine_table.reshape(slab_count, row_count, extent)
    blocked_sine = sine_table.reshape(slab_count, row_count, extent)
    real_part, imag_part = rotate(
        arrived[:, :, :, 0], arrived[:, :, :, 1], "szbgy,sgw->bzwy", blocked_cosine, blocked_sine, 1.0
    )
    plane_real, plane_imag = rotate(
        real_part, imag_part, "bzxy,yw->bzxw", cosine_kept, sine_kept, 1.0
    )
    factor = 1.0 / (float(extent) ** 3 * bands_all)
    weights = occupations * factor
    partial_value = jnp.einsum(
        "b,bzxy->zxy",
        weights,
        plane_real * plane_real + plane_imag * plane_imag,
        precision=lax.Precision.HIGHEST,
    )
    basis, frequency, weight = real_basis(extent)
    spectrum = project("zxy,mx->zmy", partial_value, basis)
    spectrum = project("zxy,my->zxm", spectrum, basis)
    arrived = lax.all_to_all(spectrum, "slab", split_axis=1, concat_axis=0, tiled=True)
    spectrum = project("zxy,mz->mxy", arrived, basis)
    kernel = real_kernel_block(extent, frequency, weight, slab_index * row_count, row_count)
    kernel = jnp.transpose(kernel, (2, 0, 1))
    potential = project("mxy,mz->zxy", kernel * spectrum, basis)
    arrived = lax.all_to_all(potential, "slab", split_axis=0, concat_axis=1, tiled=True)
    potential = project("zmy,mx->zxy", arrived, basis)
    partial_hartree = project("zxm,my->zxy", potential, basis)
    both = jnp.stack((partial_value, partial_hartree)).reshape(
        2, row_count, plane_count, half_count * band_rows, extent
    )
    summed = lax.all_to_all(both, "plane", split_axis=2, concat_axis=2, tiled=True).sum(axis=2)
    summed = summed.reshape(2, row_count, half_count, band_rows, extent)
    summed = lax.all_to_all(summed, "half", split_axis=2, concat_axis=2, tiled=True).sum(axis=2)
    placed = lax.all_to_all(summed, "slab", split_axis=3, concat_axis=1, tiled=True)
    placed = jnp.transpose(placed, (0, 2, 3, 1))
    own_density, hartree = placed[0], placed[1]
    xc_potential = exchange_correlation(own_density + core_density)
    return (hartree, xc_potential)


def solution(mesh):
    band_count, slab_count = mesh.devices.shape
    split_mesh = Mesh(
        mesh.devices.reshape(band_count // 2, 2, slab_count), ("plane", "half", "slab")
    )
    band = ("plane", "half")
    return jax.shard_map(
        local,
        mesh=split_mesh,
        in_specs=(P(band, None, "slab", None, None), P(), P(band), P(band, "slab", None)),
        out_specs=(P(band, "slab", None), P(band, "slab", None)),
        check_vma=False,
    )
```

```python
import math

import jax
import jax.numpy as jnp
from jax import lax
from jax.sharding import Mesh, PartitionSpec as P

grid_spacing = 0.59
wigner_a = 0.44
wigner_b = 7.8


def dft_tables(extent):
    indices = jnp.arange(extent, dtype=jnp.int32)
    phase = indices[:, None] * indices[None, :] % extent
    angle = phase.astype(jnp.float32) * (2.0 * math.pi / extent)
    return (jnp.cos(angle), jnp.sin(angle))


def kernel_block(extent, starts, amounts):
    pieces = []
    for offset, amount in zip(starts, amounts):
        frequency = offset + jnp.arange(amount, dtype=jnp.int32)
        shifted = (frequency + extent // 2) % extent - extent // 2
        pieces.append(shifted * shifted)
    squared = pieces[0][:, None, None] + pieces[1][None, :, None] + pieces[2][None, None, :]
    length = extent * grid_spacing
    scaled = length * length / math.pi / jnp.maximum(squared, 1).astype(jnp.float32)
    return jnp.where(squared == 0, 0.0, scaled)


def exchange_correlation(density):
    root_density = jnp.cbrt(density)
    radius = (3.0 / (4.0 * math.pi)) ** (1.0 / 3.0) / root_density
    exchange_part = -((3.0 / math.pi) ** (1.0 / 3.0)) * root_density
    shifted = radius + wigner_b
    correlation = -wigner_a / shifted - wigner_a * radius / (3.0 * shifted * shifted)
    return exchange_part + correlation


def project(pattern, values, matrix):
    return jnp.einsum(pattern, values, matrix, precision=lax.Precision.HIGH)


def rotate(real_part, imag_part, pattern, cosine_table, sine_table, direction):
    new_real = project(pattern, real_part, cosine_table) - direction * project(
        pattern, imag_part, sine_table
    )
    new_imag = direction * project(pattern, real_part, sine_table) + project(
        pattern, imag_part, cosine_table
    )
    return (new_real, new_imag)


def real_basis(extent):
    half = extent // 2
    indices = jnp.arange(extent, dtype=jnp.int32)
    frequency = jnp.where(indices <= half, indices, indices - half)
    phase = frequency[:, None] * indices[None, :] % extent
    angle = phase.astype(jnp.float32) * (2.0 * math.pi / extent)
    basis = jnp.where((indices <= half)[:, None], jnp.cos(angle), jnp.sin(angle))
    weight = jnp.where((indices == 0) | (indices == half), 1.0, 2.0).astype(jnp.float32)
    return basis, frequency, weight


def real_kernel_block(extent, frequency, weight, start, amount):
    rows = lax.dynamic_slice_in_dim(frequency, start, amount, 0)
    row_weight = lax.dynamic_slice_in_dim(weight, start, amount, 0)
    squared = (
        (rows * rows)[:, None, None]
        + (frequency * frequency)[None, :, None]
        + (frequency * frequency)[None, None, :]
    )
    length = extent * grid_spacing
    scaled = length * length / math.pi / jnp.maximum(squared, 1).astype(jnp.float32)
    kernel = jnp.where(squared == 0, 0.0, scaled)
    scale = row_weight[:, None, None] * weight[None, :, None] * weight[None, None, :]
    return kernel * scale / float(extent) ** 3


def support(values, axis, half_width):
    extent = values.shape[axis]
    low = lax.slice_in_dim(values, 0, half_width, axis=axis)
    high = lax.slice_in_dim(values, extent - half_width, extent, axis=axis)
    return jnp.concatenate((low, high), axis=axis)


def local(wave_coeffs, column_mask, occupations, core_density):
    local_bands = wave_coeffs.shape[0]
    row_count = wave_coeffs.shape[2]
    extent = wave_coeffs.shape[3]
    plane_count = lax.axis_size("plane")
    half_count = lax.axis_size("half")
    band_count = plane_count * half_count
    bands_all = band_count * local_bands
    band_rows = extent // band_count
    slab_count = lax.axis_size("slab")
    slab_index = lax.axis_index("slab")
    half_width = -(-(extent // 4 + 1) // 4) * 4
    cosine_table, sine_table = dft_tables(extent)
    cosine_kept = support(cosine_table, 0, half_width)
    sine_kept = support(sine_table, 0, half_width)
    mask_rows = lax.dynamic_slice_in_dim(column_mask, slab_index * row_count, row_count, 0)
    mask_kept = support(mask_rows, 1, half_width).astype(jnp.float32)
    masked = support(wave_coeffs, 3, half_width) * mask_kept[None, None, :, :, None]
    real_part, imag_part = rotate(
        masked[:, 0], masked[:, 1], "bxyz,zw->wbxy", cosine_table, sine_table, 1.0
    )
    stacked = jnp.stack((real_part, imag_part), axis=2).reshape(
        slab_count, extent // slab_count, -1
    )
    arrived = lax.all_to_all(stacked, "slab", split_axis=0, concat_axis=0, tiled=True)
    arrived = arrived.reshape(
        slab_count, extent // slab_count, local_bands, 2, row_count, 2 * half_width
    )
    blocked_cosine = cosine_table.reshape(slab_count, row_count, extent)
    blocked_sine = sine_table.reshape(slab_count, row_count, extent)
    real_part, imag_part = rotate(
        arrived[:, :, :, 0], arrived[:, :, :, 1], "szbgy,sgw->bzwy", blocked_cosine, blocked_sine, 1.0
    )
    plane_real, plane_imag = rotate(
        real_part, imag_part, "bzxy,yw->bzxw", cosine_kept, sine_kept, 1.0
    )
    factor = 1.0 / (float(extent) ** 3 * bands_all)
    weights = occupations * factor
    modulus = plane_real * plane_real + plane_imag * plane_imag
    partial_value = weights[0] * modulus[0]
    for member in range(1, local_bands):
        partial_value = partial_value + weights[member] * modulus[member]
    basis, frequency, weight = real_basis(extent)
    spectrum = project("zxy,mx->zmy", partial_value, basis)
    spectrum = project("zxy,my->zxm", spectrum, basis)
    arrived = lax.all_to_all(spectrum, "slab", split_axis=1, concat_axis=0, tiled=True)
    spectrum = project("zxy,mz->mxy", arrived, basis)
    kernel = real_kernel_block(extent, frequency, weight, slab_index * row_count, row_count)
    kernel = jnp.transpose(kernel, (2, 0, 1))
    potential = project("mxy,mz->zxy", kernel * spectrum, basis)
    arrived = lax.all_to_all(potential, "slab", split_axis=0, concat_axis=1, tiled=True)
    potential = project("zmy,mx->zxy", arrived, basis)
    partial_hartree = project("zxm,my->zxy", potential, basis)
    both = jnp.stack((partial_value, partial_hartree)).reshape(
        2, row_count, plane_count, half_count * band_rows, extent
    )
    summed = lax.all_to_all(both, "plane", split_axis=2, concat_axis=2, tiled=True).sum(axis=2)
    summed = summed.reshape(2, row_count, half_count, band_rows, extent)
    summed = lax.all_to_all(summed, "half", split_axis=2, concat_axis=2, tiled=True).sum(axis=2)
    placed = lax.all_to_all(summed, "slab", split_axis=3, concat_axis=1, tiled=True)
    placed = jnp.transpose(placed, (0, 2, 3, 1))
    own_density, hartree = placed[0], placed[1]
    xc_potential = exchange_correlation(own_density + core_density)
    return (hartree, xc_potential)


def solution(mesh):
    band_count, slab_count = mesh.devices.shape
    split_mesh = Mesh(
        mesh.devices.reshape(band_count // 2, 2, slab_count), ("plane", "half", "slab")
    )
    band = ("plane", "half")
    return jax.shard_map(
        local,
        mesh=split_mesh,
        in_specs=(P(band, None, "slab", None, None), P(), P(band), P(band, "slab", None)),
        out_specs=(P(band, "slab", None), P(band, "slab", None)),
        check_vma=False,
    )
```

```python
import math

import jax
import jax.numpy as jnp
from jax import lax
from jax.sharding import Mesh, PartitionSpec as P

grid_spacing = 0.59
wigner_a = 0.44
wigner_b = 7.8


def dft_tables(extent):
    indices = jnp.arange(extent, dtype=jnp.int32)
    phase = indices[:, None] * indices[None, :] % extent
    angle = phase.astype(jnp.float32) * (2.0 * math.pi / extent)
    return (jnp.cos(angle), jnp.sin(angle))


def kernel_block(extent, starts, amounts):
    pieces = []
    for offset, amount in zip(starts, amounts):
        frequency = offset + jnp.arange(amount, dtype=jnp.int32)
        shifted = (frequency + extent // 2) % extent - extent // 2
        pieces.append(shifted * shifted)
    squared = pieces[0][:, None, None] + pieces[1][None, :, None] + pieces[2][None, None, :]
    length = extent * grid_spacing
    scaled = length * length / math.pi / jnp.maximum(squared, 1).astype(jnp.float32)
    return jnp.where(squared == 0, 0.0, scaled)


def exchange_correlation(density):
    root_density = jnp.cbrt(density)
    radius = (3.0 / (4.0 * math.pi)) ** (1.0 / 3.0) / root_density
    exchange_part = -((3.0 / math.pi) ** (1.0 / 3.0)) * root_density
    shifted = radius + wigner_b
    correlation = -wigner_a / shifted - wigner_a * radius / (3.0 * shifted * shifted)
    return exchange_part + correlation


def project(pattern, values, matrix, precision=lax.Precision.HIGHEST):
    return jnp.einsum(pattern, values, matrix, precision=precision)


def rotate(real_part, imag_part, pattern, cosine_table, sine_table, direction):
    fast = lax.Precision.HIGH
    new_real = project(pattern, real_part, cosine_table, fast) - direction * project(
        pattern, imag_part, sine_table, fast
    )
    new_imag = direction * project(pattern, real_part, sine_table, fast) + project(
        pattern, imag_part, cosine_table, fast
    )
    return (new_real, new_imag)


def real_basis(extent):
    half = extent // 2
    indices = jnp.arange(extent, dtype=jnp.int32)
    frequency = jnp.where(indices <= half, indices, indices - half)
    phase = frequency[:, None] * indices[None, :] % extent
    angle = phase.astype(jnp.float32) * (2.0 * math.pi / extent)
    basis = jnp.where((indices <= half)[:, None], jnp.cos(angle), jnp.sin(angle))
    weight = jnp.where((indices == 0) | (indices == half), 1.0, 2.0).astype(jnp.float32)
    return basis, frequency, weight


def real_kernel_block(extent, frequency, weight, start, amount):
    rows = lax.dynamic_slice_in_dim(frequency, start, amount, 0)
    row_weight = lax.dynamic_slice_in_dim(weight, start, amount, 0)
    squared = (
        (rows * rows)[:, None, None]
        + (frequency * frequency)[None, :, None]
        + (frequency * frequency)[None, None, :]
    )
    length = extent * grid_spacing
    scaled = length * length / math.pi / jnp.maximum(squared, 1).astype(jnp.float32)
    kernel = jnp.where(squared == 0, 0.0, scaled)
    scale = row_weight[:, None, None] * weight[None, :, None] * weight[None, None, :]
    return kernel * scale / float(extent) ** 3


def support(values, axis, half_width):
    extent = values.shape[axis]
    low = lax.slice_in_dim(values, 0, half_width, axis=axis)
    high = lax.slice_in_dim(values, extent - half_width, extent, axis=axis)
    return jnp.concatenate((low, high), axis=axis)


def local(wave_coeffs, column_mask, occupations, core_density):
    local_bands = wave_coeffs.shape[0]
    row_count = wave_coeffs.shape[2]
    extent = wave_coeffs.shape[3]
    plane_count = lax.axis_size("plane")
    half_count = lax.axis_size("half")
    band_count = plane_count * half_count
    bands_all = band_count * local_bands
    band_rows = extent // band_count
    slab_count = lax.axis_size("slab")
    slab_index = lax.axis_index("slab")
    half_width = -(-(extent // 4 + 1) // 4) * 4
    cosine_table, sine_table = dft_tables(extent)
    cosine_kept = support(cosine_table, 0, half_width)
    sine_kept = support(sine_table, 0, half_width)
    mask_rows = lax.dynamic_slice_in_dim(column_mask, slab_index * row_count, row_count, 0)
    mask_kept = support(mask_rows, 1, half_width).astype(jnp.float32)
    masked = support(wave_coeffs, 3, half_width) * mask_kept[None, None, :, :, None]
    real_part, imag_part = rotate(
        masked[:, 0], masked[:, 1], "bxyz,zw->wbxy", cosine_table, sine_table, 1.0
    )
    stacked = jnp.stack((real_part, imag_part), axis=2).reshape(
        slab_count, extent // slab_count, -1
    )
    arrived = lax.all_to_all(stacked, "slab", split_axis=0, concat_axis=0, tiled=True)
    arrived = arrived.reshape(
        slab_count, extent // slab_count, local_bands, 2, row_count, 2 * half_width
    )
    blocked_cosine = cosine_table.reshape(slab_count, row_count, extent)
    blocked_sine = sine_table.reshape(slab_count, row_count, extent)
    real_part, imag_part = rotate(
        arrived[:, :, :, 0], arrived[:, :, :, 1], "szbgy,sgw->bzwy", blocked_cosine, blocked_sine, 1.0
    )
    plane_real, plane_imag = rotate(
        real_part, imag_part, "bzxy,yw->bzxw", cosine_kept, sine_kept, 1.0
    )
    factor = 1.0 / (float(extent) ** 3 * bands_all)
    weights = occupations * factor
    modulus = plane_real * plane_real + plane_imag * plane_imag
    partial_value = weights[0] * modulus[0]
    for member in range(1, local_bands):
        partial_value = partial_value + weights[member] * modulus[member]
    basis, frequency, weight = real_basis(extent)
    spectrum = project("zxy,mx->zmy", partial_value, basis)
    spectrum = project("zxy,my->zxm", spectrum, basis)
    arrived = lax.all_to_all(spectrum, "slab", split_axis=1, concat_axis=0, tiled=True)
    spectrum = project("zxy,mz->mxy", arrived, basis)
    kernel = real_kernel_block(extent, frequency, weight, slab_index * row_count, row_count)
    kernel = jnp.transpose(kernel, (2, 0, 1))
    potential = project("mxy,mz->zxy", kernel * spectrum, basis)
    arrived = lax.all_to_all(potential, "slab", split_axis=0, concat_axis=1, tiled=True)
    potential = project("zmy,mx->zxy", arrived, basis)
    partial_hartree = project("zxm,my->zxy", potential, basis)
    both = jnp.stack((partial_value, partial_hartree)).reshape(
        2, row_count, plane_count, half_count * band_rows, extent
    )
    summed = lax.all_to_all(both, "plane", split_axis=2, concat_axis=2, tiled=True).sum(axis=2)
    summed = summed.reshape(2, row_count, half_count, band_rows, slab_count, row_count)
    summed = jnp.transpose(summed, (2, 4, 0, 1, 3, 5)).reshape(
        half_count * slab_count, 2, row_count, band_rows, row_count
    )
    arrived = lax.all_to_all(summed, ("half", "slab"), split_axis=0, concat_axis=0, tiled=True)
    arrived = arrived.reshape(half_count, slab_count, 2, row_count, band_rows, row_count).sum(axis=0)
    placed = jnp.transpose(arrived, (1, 3, 4, 0, 2)).reshape(2, band_rows, row_count, extent)
    own_density, hartree = placed[0], placed[1]
    xc_potential = exchange_correlation(own_density + core_density)
    return (hartree, xc_potential)


def solution(mesh):
    band_count, slab_count = mesh.devices.shape
    split_mesh = Mesh(
        mesh.devices.reshape(band_count // 2, 2, slab_count), ("plane", "half", "slab")
    )
    band = ("plane", "half")
    return jax.shard_map(
        local,
        mesh=split_mesh,
        in_specs=(P(band, None, "slab", None, None), P(), P(band), P(band, "slab", None)),
        out_specs=(P(band, "slab", None), P(band, "slab", None)),
        check_vma=False,
    )
```

```python
import math

import jax
import jax.numpy as jnp
from jax import lax
from jax.sharding import Mesh, PartitionSpec as P

grid_spacing = 0.59
wigner_a = 0.44
wigner_b = 7.8


def dft_tables(extent):
    indices = jnp.arange(extent, dtype=jnp.int32)
    phase = indices[:, None] * indices[None, :] % extent
    angle = phase.astype(jnp.float32) * (2.0 * math.pi / extent)
    return (jnp.cos(angle), jnp.sin(angle))


def kernel_block(extent, starts, amounts):
    pieces = []
    for offset, amount in zip(starts, amounts):
        frequency = offset + jnp.arange(amount, dtype=jnp.int32)
        shifted = (frequency + extent // 2) % extent - extent // 2
        pieces.append(shifted * shifted)
    squared = pieces[0][:, None, None] + pieces[1][None, :, None] + pieces[2][None, None, :]
    length = extent * grid_spacing
    scaled = length * length / math.pi / jnp.maximum(squared, 1).astype(jnp.float32)
    return jnp.where(squared == 0, 0.0, scaled)


def exchange_correlation(density):
    root_density = jnp.cbrt(density)
    radius = (3.0 / (4.0 * math.pi)) ** (1.0 / 3.0) / root_density
    exchange_part = -((3.0 / math.pi) ** (1.0 / 3.0)) * root_density
    shifted = radius + wigner_b
    correlation = -wigner_a / shifted - wigner_a * radius / (3.0 * shifted * shifted)
    return exchange_part + correlation


def project(pattern, values, matrix, precision=lax.Precision.HIGHEST):
    return jnp.einsum(pattern, values, matrix, precision=precision)


def rotate(real_part, imag_part, pattern, cosine_table, sine_table, direction):
    fast = lax.Precision.HIGH
    new_real = project(pattern, real_part, cosine_table, fast) - direction * project(
        pattern, imag_part, sine_table, fast
    )
    new_imag = direction * project(pattern, real_part, sine_table, fast) + project(
        pattern, imag_part, cosine_table, fast
    )
    return (new_real, new_imag)


def real_basis(extent):
    half = extent // 2
    indices = jnp.arange(extent, dtype=jnp.int32)
    frequency = jnp.where(indices <= half, indices, indices - half)
    phase = frequency[:, None] * indices[None, :] % extent
    angle = phase.astype(jnp.float32) * (2.0 * math.pi / extent)
    basis = jnp.where((indices <= half)[:, None], jnp.cos(angle), jnp.sin(angle))
    weight = jnp.where((indices == 0) | (indices == half), 1.0, 2.0).astype(jnp.float32)
    return basis, frequency, weight


def real_kernel_block(extent, frequency, weight, start, amount):
    rows = lax.dynamic_slice_in_dim(frequency, start, amount, 0)
    row_weight = lax.dynamic_slice_in_dim(weight, start, amount, 0)
    squared = (
        (rows * rows)[:, None, None]
        + (frequency * frequency)[None, :, None]
        + (frequency * frequency)[None, None, :]
    )
    length = extent * grid_spacing
    scaled = length * length / math.pi / jnp.maximum(squared, 1).astype(jnp.float32)
    kernel = jnp.where(squared == 0, 0.0, scaled)
    scale = row_weight[:, None, None] * weight[None, :, None] * weight[None, None, :]
    return kernel * scale / float(extent) ** 3


def support(values, axis, half_width):
    extent = values.shape[axis]
    low = lax.slice_in_dim(values, 0, half_width, axis=axis)
    high = lax.slice_in_dim(values, extent - half_width, extent, axis=axis)
    return jnp.concatenate((low, high), axis=axis)


def keep_slabs(values, live):
    runs = []
    for slab in live:
        if runs and runs[-1][1] == slab:
            runs[-1][1] = slab + 1
        else:
            runs.append([slab, slab + 1])
    pieces = [values[start:stop] for start, stop in runs]
    return pieces[0] if len(pieces) == 1 else jnp.concatenate(pieces, axis=0)


def local(wave_coeffs, column_mask, occupations, core_density):
    local_bands = wave_coeffs.shape[0]
    row_count = wave_coeffs.shape[2]
    extent = wave_coeffs.shape[3]
    plane_count = lax.axis_size("plane")
    half_count = lax.axis_size("half")
    band_count = plane_count * half_count
    bands_all = band_count * local_bands
    band_rows = extent // band_count
    slab_count = lax.axis_size("slab")
    slab_index = lax.axis_index("slab")
    half_width = -(-(extent // 4 + 1) // 4) * 4
    cosine_table, sine_table = dft_tables(extent)
    cosine_kept = support(cosine_table, 0, half_width)
    sine_kept = support(sine_table, 0, half_width)
    mask_rows = lax.dynamic_slice_in_dim(column_mask, slab_index * row_count, row_count, 0)
    mask_kept = support(mask_rows, 1, half_width).astype(jnp.float32)
    masked = support(wave_coeffs, 3, half_width) * mask_kept[None, None, :, :, None]
    real_part, imag_part = rotate(
        masked[:, 0], masked[:, 1], "bxyz,zw->wbxy", cosine_table, sine_table, 1.0
    )
    stacked = jnp.stack((real_part, imag_part), axis=2).reshape(
        slab_count, extent // slab_count, -1
    )
    arrived = lax.all_to_all(stacked, "slab", split_axis=0, concat_axis=0, tiled=True)
    arrived = arrived.reshape(
        slab_count, extent // slab_count, local_bands, 2, row_count, 2 * half_width
    )
    blocked_cosine = cosine_table.reshape(slab_count, row_count, extent)
    blocked_sine = sine_table.reshape(slab_count, row_count, extent)
    live = [
        slab
        for slab in range(slab_count)
        if any(
            abs((row + extent // 2) % extent - extent // 2) <= extent // 4
            for row in range(slab * row_count, (slab + 1) * row_count)
        )
    ]
    arrived = keep_slabs(arrived, live)
    blocked_cosine = keep_slabs(blocked_cosine, live)
    blocked_sine = keep_slabs(blocked_sine, live)
    real_part, imag_part = rotate(
        arrived[:, :, :, 0], arrived[:, :, :, 1], "szbgy,sgw->bzwy", blocked_cosine, blocked_sine, 1.0
    )
    plane_real, plane_imag = rotate(
        real_part, imag_part, "bzxy,yw->bzxw", cosine_kept, sine_kept, 1.0
    )
    factor = 1.0 / (float(extent) ** 3 * bands_all)
    weights = occupations * factor
    modulus = plane_real * plane_real + plane_imag * plane_imag
    partial_value = weights[0] * modulus[0]
    for member in range(1, local_bands):
        partial_value = partial_value + weights[member] * modulus[member]
    basis, frequency, weight = real_basis(extent)
    spectrum = project("zxy,mx->mzy", partial_value, basis)
    spectrum = project("xzy,my->xzm", spectrum, basis)
    arrived = lax.all_to_all(spectrum, "slab", split_axis=0, concat_axis=1, tiled=True)
    spectrum = project("xzy,mz->mxy", arrived, basis)
    kernel = real_kernel_block(extent, frequency, weight, slab_index * row_count, row_count)
    kernel = jnp.transpose(kernel, (2, 0, 1))
    potential = project("mxy,mz->zxy", kernel * spectrum, basis)
    arrived = lax.all_to_all(potential, "slab", split_axis=0, concat_axis=1, tiled=True)
    potential = project("zmy,mx->zxy", arrived, basis)
    partial_hartree = project("zxm,my->zxy", potential, basis)
    both = jnp.stack((partial_value, partial_hartree)).reshape(
        2, row_count, plane_count, half_count * band_rows, extent
    )
    summed = lax.all_to_all(both, "plane", split_axis=2, concat_axis=2, tiled=True).sum(axis=2)
    summed = summed.reshape(2, row_count, half_count, band_rows, slab_count, row_count)
    summed = jnp.transpose(summed, (2, 4, 0, 1, 3, 5)).reshape(
        half_count * slab_count, 2, row_count, band_rows, row_count
    )
    arrived = lax.all_to_all(summed, ("half", "slab"), split_axis=0, concat_axis=0, tiled=True)
    arrived = arrived.reshape(half_count, slab_count, 2, row_count, band_rows, row_count).sum(axis=0)
    placed = jnp.transpose(arrived, (1, 3, 4, 0, 2)).reshape(2, band_rows, row_count, extent)
    own_density, hartree = placed[0], placed[1]
    xc_potential = exchange_correlation(own_density + core_density)
    return (hartree, xc_potential)


def solution(mesh):
    band_count, slab_count = mesh.devices.shape
    split_mesh = Mesh(
        mesh.devices.reshape(band_count // 2, 2, slab_count), ("plane", "half", "slab")
    )
    band = ("plane", "half")
    return jax.shard_map(
        local,
        mesh=split_mesh,
        in_specs=(P(band, None, "slab", None, None), P(), P(band), P(band, "slab", None)),
        out_specs=(P(band, "slab", None), P(band, "slab", None)),
        check_vma=False,
    )
```

```python
import math

import jax
import jax.numpy as jnp
from jax import lax
from jax.sharding import Mesh, PartitionSpec as P

grid_spacing = 0.59
wigner_a = 0.44
wigner_b = 7.8


def dft_tables(extent):
    indices = jnp.arange(extent, dtype=jnp.int32)
    phase = indices[:, None] * indices[None, :] % extent
    angle = phase.astype(jnp.float32) * (2.0 * math.pi / extent)
    return (jnp.cos(angle), jnp.sin(angle))


def kernel_block(extent, starts, amounts):
    pieces = []
    for offset, amount in zip(starts, amounts):
        frequency = offset + jnp.arange(amount, dtype=jnp.int32)
        shifted = (frequency + extent // 2) % extent - extent // 2
        pieces.append(shifted * shifted)
    squared = pieces[0][:, None, None] + pieces[1][None, :, None] + pieces[2][None, None, :]
    length = extent * grid_spacing
    scaled = length * length / math.pi / jnp.maximum(squared, 1).astype(jnp.float32)
    return jnp.where(squared == 0, 0.0, scaled)


def exchange_correlation(density):
    root_density = jnp.cbrt(density)
    radius = (3.0 / (4.0 * math.pi)) ** (1.0 / 3.0) / root_density
    exchange_part = -((3.0 / math.pi) ** (1.0 / 3.0)) * root_density
    shifted = radius + wigner_b
    correlation = -wigner_a / shifted - wigner_a * radius / (3.0 * shifted * shifted)
    return exchange_part + correlation


def project(pattern, values, matrix, precision=lax.Precision.HIGHEST):
    return jnp.einsum(pattern, values, matrix, precision=precision)


def rotate(real_part, imag_part, pattern, cosine_table, sine_table, direction):
    fast = lax.Precision.HIGH
    new_real = project(pattern, real_part, cosine_table, fast) - direction * project(
        pattern, imag_part, sine_table, fast
    )
    new_imag = direction * project(pattern, real_part, sine_table, fast) + project(
        pattern, imag_part, cosine_table, fast
    )
    return (new_real, new_imag)


def real_basis(extent):
    half = extent // 2
    indices = jnp.arange(extent, dtype=jnp.int32)
    frequency = jnp.where(indices <= half, indices, indices - half)
    phase = frequency[:, None] * indices[None, :] % extent
    angle = phase.astype(jnp.float32) * (2.0 * math.pi / extent)
    basis = jnp.where((indices <= half)[:, None], jnp.cos(angle), jnp.sin(angle))
    weight = jnp.where((indices == 0) | (indices == half), 1.0, 2.0).astype(jnp.float32)
    return basis, frequency, weight


def real_kernel_block(extent, frequency, weight, start, amount):
    rows = lax.dynamic_slice_in_dim(frequency, start, amount, 0)
    row_weight = lax.dynamic_slice_in_dim(weight, start, amount, 0)
    squared = (
        (rows * rows)[:, None, None]
        + (frequency * frequency)[None, :, None]
        + (frequency * frequency)[None, None, :]
    )
    length = extent * grid_spacing
    scaled = length * length / math.pi / jnp.maximum(squared, 1).astype(jnp.float32)
    kernel = jnp.where(squared == 0, 0.0, scaled)
    scale = row_weight[:, None, None] * weight[None, :, None] * weight[None, None, :]
    return kernel * scale / float(extent) ** 3


def support(values, axis, half_width):
    extent = values.shape[axis]
    low = lax.slice_in_dim(values, 0, half_width, axis=axis)
    high = lax.slice_in_dim(values, extent - half_width, extent, axis=axis)
    return jnp.concatenate((low, high), axis=axis)


def keep_slabs(values, live):
    runs = []
    for slab in live:
        if runs and runs[-1][1] == slab:
            runs[-1][1] = slab + 1
        else:
            runs.append([slab, slab + 1])
    pieces = [values[start:stop] for start, stop in runs]
    return pieces[0] if len(pieces) == 1 else jnp.concatenate(pieces, axis=0)


def exchange(values, axis_name, split_axis, concat_axis):
    count = lax.axis_size(axis_name)
    shape = values.shape
    chunk = shape[split_axis] // count
    parts = values.reshape(shape[:split_axis] + (count, chunk) + shape[split_axis + 1 :])
    parts = jnp.moveaxis(parts, split_axis, 0)
    inner = parts.shape[1:]
    parts = lax.all_to_all(parts.reshape(count, -1), axis_name, 0, 0, tiled=True)
    parts = jnp.moveaxis(parts.reshape((count,) + inner), 0, concat_axis)
    merged = list(inner)
    merged[concat_axis] *= count
    return parts.reshape(merged)


def block_kernel(extent, frequency, weight, first, second):
    rows_a = lax.dynamic_slice_in_dim(frequency, first[0], first[1], 0)
    rows_b = lax.dynamic_slice_in_dim(frequency, second[0], second[1], 0)
    weight_a = lax.dynamic_slice_in_dim(weight, first[0], first[1], 0)
    weight_b = lax.dynamic_slice_in_dim(weight, second[0], second[1], 0)
    squared = (
        (frequency * frequency)[:, None, None]
        + (rows_a * rows_a)[None, :, None]
        + (rows_b * rows_b)[None, None, :]
    )
    length = extent * grid_spacing
    scaled = length * length / math.pi / jnp.maximum(squared, 1).astype(jnp.float32)
    kernel = jnp.where(squared == 0, 0.0, scaled)
    scale = weight[:, None, None] * weight_a[None, :, None] * weight_b[None, None, :]
    return kernel * scale / float(extent) ** 3


def local(wave_coeffs, column_mask, occupations, core_density):
    local_bands = wave_coeffs.shape[0]
    row_count = wave_coeffs.shape[2]
    extent = wave_coeffs.shape[3]
    plane_count = lax.axis_size("plane")
    half_count = lax.axis_size("half")
    band_count = plane_count * half_count
    bands_all = band_count * local_bands
    band_rows = extent // band_count
    slab_count = lax.axis_size("slab")
    slab_index = lax.axis_index("slab")
    half_width = -(-(extent // 4 + 1) // 4) * 4
    cosine_table, sine_table = dft_tables(extent)
    cosine_kept = support(cosine_table, 0, half_width)
    sine_kept = support(sine_table, 0, half_width)
    mask_rows = lax.dynamic_slice_in_dim(column_mask, slab_index * row_count, row_count, 0)
    mask_kept = support(mask_rows, 1, half_width).astype(jnp.float32)
    masked = support(wave_coeffs, 3, half_width) * mask_kept[None, None, :, :, None]
    real_part, imag_part = rotate(
        masked[:, 0], masked[:, 1], "bxyz,zw->wbxy", cosine_table, sine_table, 1.0
    )
    stacked = jnp.stack((real_part, imag_part), axis=2).reshape(
        slab_count, extent // slab_count, -1
    )
    arrived = lax.all_to_all(stacked, "slab", split_axis=0, concat_axis=0, tiled=True)
    arrived = arrived.reshape(
        slab_count, extent // slab_count, local_bands, 2, row_count, 2 * half_width
    )
    blocked_cosine = cosine_table.reshape(slab_count, row_count, extent)
    blocked_sine = sine_table.reshape(slab_count, row_count, extent)
    live = [
        slab
        for slab in range(slab_count)
        if any(
            abs((row + extent // 2) % extent - extent // 2) <= extent // 4
            for row in range(slab * row_count, (slab + 1) * row_count)
        )
    ]
    arrived = keep_slabs(arrived, live)
    blocked_cosine = keep_slabs(blocked_cosine, live)
    blocked_sine = keep_slabs(blocked_sine, live)
    real_part, imag_part = rotate(
        arrived[:, :, :, 0], arrived[:, :, :, 1], "szbgy,sgw->bzwy", blocked_cosine, blocked_sine, 1.0
    )
    plane_real, plane_imag = rotate(
        real_part, imag_part, "bzxy,yw->bzxw", cosine_kept, sine_kept, 1.0
    )
    factor = 1.0 / (float(extent) ** 3 * bands_all)
    weights = occupations * factor
    modulus = plane_real * plane_real + plane_imag * plane_imag
    partial_value = weights[0] * modulus[0]
    for member in range(1, local_bands):
        partial_value = partial_value + weights[member] * modulus[member]
    basis, frequency, weight = real_basis(extent)
    plane_rows = half_count * band_rows
    spread = partial_value.reshape(row_count, plane_count, plane_rows, extent)
    density = lax.all_to_all(spread, "plane", split_axis=1, concat_axis=1, tiled=True).sum(axis=1)
    spectrum = project("zxy,my->zxm", density, basis)
    spectrum = exchange(spectrum, "plane", 2, 1)
    spectrum = project("zxm,nx->znm", spectrum, basis)
    spectrum = exchange(spectrum, "slab", 1, 0)
    spectrum = project("zab,mz->mab", spectrum, basis)
    plane_index = lax.axis_index("plane")
    kernel = block_kernel(
        extent,
        frequency,
        weight,
        (slab_index * row_count, row_count),
        (plane_index * (extent // plane_count), extent // plane_count),
    )
    potential = project("mab,mz->zab", kernel * spectrum, basis)
    potential = exchange(potential, "slab", 0, 1)
    potential = project("znm,nx->zxm", potential, basis)
    potential = exchange(potential, "plane", 1, 2)
    potential = project("zxm,my->zxy", potential, basis)
    summed = jnp.stack((density, potential))
    summed = summed.reshape(2, row_count, half_count, band_rows, slab_count, row_count)
    summed = jnp.transpose(summed, (2, 4, 0, 1, 3, 5)).reshape(
        half_count * slab_count, 2, row_count, band_rows, row_count
    )
    arrived = lax.all_to_all(summed, ("half", "slab"), split_axis=0, concat_axis=0, tiled=True)
    arrived = arrived.reshape(half_count, slab_count, 2, row_count, band_rows, row_count).sum(axis=0)
    placed = jnp.transpose(arrived, (1, 3, 4, 0, 2)).reshape(2, band_rows, row_count, extent)
    own_density, hartree = placed[0], placed[1]
    xc_potential = exchange_correlation(own_density + core_density)
    return (hartree, xc_potential)


def solution(mesh):
    band_count, slab_count = mesh.devices.shape
    split_mesh = Mesh(
        mesh.devices.reshape(band_count // 2, 2, slab_count), ("plane", "half", "slab")
    )
    band = ("plane", "half")
    return jax.shard_map(
        local,
        mesh=split_mesh,
        in_specs=(P(band, None, "slab", None, None), P(), P(band), P(band, "slab", None)),
        out_specs=(P(band, "slab", None), P(band, "slab", None)),
        check_vma=False,
    )
```

```python
import math

import jax
import jax.numpy as jnp
from jax import lax
from jax.sharding import Mesh, PartitionSpec as P

grid_spacing = 0.59
wigner_a = 0.44
wigner_b = 7.8


def dft_tables(extent):
    indices = jnp.arange(extent, dtype=jnp.int32)
    phase = indices[:, None] * indices[None, :] % extent
    angle = phase.astype(jnp.float32) * (2.0 * math.pi / extent)
    return (jnp.cos(angle), jnp.sin(angle))


def kernel_block(extent, starts, amounts):
    pieces = []
    for offset, amount in zip(starts, amounts):
        frequency = offset + jnp.arange(amount, dtype=jnp.int32)
        shifted = (frequency + extent // 2) % extent - extent // 2
        pieces.append(shifted * shifted)
    squared = pieces[0][:, None, None] + pieces[1][None, :, None] + pieces[2][None, None, :]
    length = extent * grid_spacing
    scaled = length * length / math.pi / jnp.maximum(squared, 1).astype(jnp.float32)
    return jnp.where(squared == 0, 0.0, scaled)


def exchange_correlation(density):
    root_density = jnp.cbrt(density)
    radius = (3.0 / (4.0 * math.pi)) ** (1.0 / 3.0) / root_density
    exchange_part = -((3.0 / math.pi) ** (1.0 / 3.0)) * root_density
    shifted = radius + wigner_b
    correlation = -wigner_a / shifted - wigner_a * radius / (3.0 * shifted * shifted)
    return exchange_part + correlation


def project(pattern, values, matrix, precision=lax.Precision.HIGHEST):
    return jnp.einsum(pattern, values, matrix, precision=precision)


def rotate(real_part, imag_part, pattern, cosine_table, sine_table, direction):
    fast = lax.Precision.HIGH
    new_real = project(pattern, real_part, cosine_table, fast) - direction * project(
        pattern, imag_part, sine_table, fast
    )
    new_imag = direction * project(pattern, real_part, sine_table, fast) + project(
        pattern, imag_part, cosine_table, fast
    )
    return (new_real, new_imag)


def real_basis(extent):
    half = extent // 2
    indices = jnp.arange(extent, dtype=jnp.int32)
    frequency = jnp.where(indices <= half, indices, indices - half)
    phase = frequency[:, None] * indices[None, :] % extent
    angle = phase.astype(jnp.float32) * (2.0 * math.pi / extent)
    basis = jnp.where((indices <= half)[:, None], jnp.cos(angle), jnp.sin(angle))
    weight = jnp.where((indices == 0) | (indices == half), 1.0, 2.0).astype(jnp.float32)
    return basis, frequency, weight


def real_kernel_block(extent, frequency, weight, start, amount):
    rows = lax.dynamic_slice_in_dim(frequency, start, amount, 0)
    row_weight = lax.dynamic_slice_in_dim(weight, start, amount, 0)
    squared = (
        (rows * rows)[:, None, None]
        + (frequency * frequency)[None, :, None]
        + (frequency * frequency)[None, None, :]
    )
    length = extent * grid_spacing
    scaled = length * length / math.pi / jnp.maximum(squared, 1).astype(jnp.float32)
    kernel = jnp.where(squared == 0, 0.0, scaled)
    scale = row_weight[:, None, None] * weight[None, :, None] * weight[None, None, :]
    return kernel * scale / float(extent) ** 3


def support(values, axis, radius):
    extent = values.shape[axis]
    low = lax.slice_in_dim(values, 0, radius + 1, axis=axis)
    high = lax.slice_in_dim(values, extent - radius, extent, axis=axis)
    return jnp.concatenate((low, high), axis=axis)


def keep_slabs(values, live):
    runs = []
    for slab in live:
        if runs and runs[-1][1] == slab:
            runs[-1][1] = slab + 1
        else:
            runs.append([slab, slab + 1])
    pieces = [values[start:stop] for start, stop in runs]
    return pieces[0] if len(pieces) == 1 else jnp.concatenate(pieces, axis=0)


def exchange(values, axis_name, split_axis, concat_axis):
    count = lax.axis_size(axis_name)
    shape = values.shape
    chunk = shape[split_axis] // count
    parts = values.reshape(shape[:split_axis] + (count, chunk) + shape[split_axis + 1 :])
    parts = jnp.moveaxis(parts, split_axis, 0)
    inner = parts.shape[1:]
    parts = lax.all_to_all(parts.reshape(count, -1), axis_name, 0, 0, tiled=True)
    parts = jnp.moveaxis(parts.reshape((count,) + inner), 0, concat_axis)
    merged = list(inner)
    merged[concat_axis] *= count
    return parts.reshape(merged)


def block_kernel(extent, frequency, weight, first, second):
    rows_a = lax.dynamic_slice_in_dim(frequency, first[0], first[1], 0)
    rows_b = lax.dynamic_slice_in_dim(frequency, second[0], second[1], 0)
    weight_a = lax.dynamic_slice_in_dim(weight, first[0], first[1], 0)
    weight_b = lax.dynamic_slice_in_dim(weight, second[0], second[1], 0)
    squared = (
        (frequency * frequency)[:, None, None]
        + (rows_a * rows_a)[None, :, None]
        + (rows_b * rows_b)[None, None, :]
    )
    length = extent * grid_spacing
    scaled = length * length / math.pi / jnp.maximum(squared, 1).astype(jnp.float32)
    kernel = jnp.where(squared == 0, 0.0, scaled)
    scale = weight[:, None, None] * weight_a[None, :, None] * weight_b[None, None, :]
    return kernel * scale / float(extent) ** 3


def local(wave_coeffs, column_mask, occupations, core_density):
    local_bands = wave_coeffs.shape[0]
    row_count = wave_coeffs.shape[2]
    extent = wave_coeffs.shape[3]
    plane_count = lax.axis_size("plane")
    half_count = lax.axis_size("half")
    band_count = plane_count * half_count
    bands_all = band_count * local_bands
    band_rows = extent // band_count
    slab_count = lax.axis_size("slab")
    slab_index = lax.axis_index("slab")
    radius = extent // 4
    cosine_table, sine_table = dft_tables(extent)
    cosine_kept = support(cosine_table, 0, radius)
    sine_kept = support(sine_table, 0, radius)
    mask_rows = lax.dynamic_slice_in_dim(column_mask, slab_index * row_count, row_count, 0)
    mask_kept = support(mask_rows, 1, radius).astype(jnp.float32)
    masked = support(wave_coeffs, 3, radius) * mask_kept[None, None, :, :, None]
    real_part, imag_part = rotate(
        masked[:, 0], masked[:, 1], "bxyz,zw->wbxy", cosine_table, sine_table, 1.0
    )
    stacked = jnp.stack((real_part, imag_part), axis=2).reshape(slab_count, -1)
    arrived = lax.all_to_all(stacked, "slab", split_axis=0, concat_axis=0, tiled=True)
    arrived = arrived.reshape(
        slab_count, extent // slab_count, local_bands, 2, row_count, 2 * radius + 1
    )
    blocked_cosine = cosine_table.reshape(slab_count, row_count, extent)
    blocked_sine = sine_table.reshape(slab_count, row_count, extent)
    live = [
        slab
        for slab in range(slab_count)
        if any(
            abs((row + extent // 2) % extent - extent // 2) <= extent // 4
            for row in range(slab * row_count, (slab + 1) * row_count)
        )
    ]
    arrived = keep_slabs(arrived, live)
    blocked_cosine = keep_slabs(blocked_cosine, live)
    blocked_sine = keep_slabs(blocked_sine, live)
    real_part, imag_part = rotate(
        arrived[:, :, :, 0], arrived[:, :, :, 1], "szbgy,sgw->bzwy", blocked_cosine, blocked_sine, 1.0
    )
    plane_real, plane_imag = rotate(
        real_part, imag_part, "bzxy,yw->bzxw", cosine_kept, sine_kept, 1.0
    )
    factor = 1.0 / (float(extent) ** 3 * bands_all)
    weights = occupations * factor
    modulus = plane_real * plane_real + plane_imag * plane_imag
    partial_value = weights[0] * modulus[0]
    for member in range(1, local_bands):
        partial_value = partial_value + weights[member] * modulus[member]
    basis, frequency, weight = real_basis(extent)
    plane_rows = half_count * band_rows
    spread = partial_value.reshape(row_count, plane_count, plane_rows, extent)
    density = lax.all_to_all(spread, "plane", split_axis=1, concat_axis=1, tiled=True).sum(axis=1)
    spectrum = project("zxy,my->zxm", density, basis)
    spectrum = exchange(spectrum, "plane", 2, 1)
    spectrum = project("zxm,nx->znm", spectrum, basis)
    spectrum = exchange(spectrum, "slab", 1, 0)
    spectrum = project("zab,mz->mab", spectrum, basis)
    plane_index = lax.axis_index("plane")
    kernel = block_kernel(
        extent,
        frequency,
        weight,
        (slab_index * row_count, row_count),
        (plane_index * (extent // plane_count), extent // plane_count),
    )
    potential = project("mab,mz->zab", kernel * spectrum, basis)
    potential = exchange(potential, "slab", 0, 1)
    potential = project("znm,nx->zxm", potential, basis)
    potential = exchange(potential, "plane", 1, 2)
    potential = project("zxm,my->zxy", potential, basis)
    summed = jnp.stack((density, potential))
    summed = summed.reshape(2, row_count, half_count, band_rows, slab_count, row_count)
    summed = jnp.transpose(summed, (2, 4, 0, 1, 3, 5)).reshape(
        half_count * slab_count, 2, row_count, band_rows, row_count
    )
    arrived = lax.all_to_all(summed, ("half", "slab"), split_axis=0, concat_axis=0, tiled=True)
    arrived = arrived.reshape(half_count, slab_count, 2, row_count, band_rows, row_count).sum(axis=0)
    placed = jnp.transpose(arrived, (1, 3, 4, 0, 2)).reshape(2, band_rows, row_count, extent)
    own_density, hartree = placed[0], placed[1]
    xc_potential = exchange_correlation(own_density + core_density)
    return (hartree, xc_potential)


def solution(mesh):
    band_count, slab_count = mesh.devices.shape
    split_mesh = Mesh(
        mesh.devices.reshape(band_count // 2, 2, slab_count), ("plane", "half", "slab")
    )
    band = ("plane", "half")
    return jax.shard_map(
        local,
        mesh=split_mesh,
        in_specs=(P(band, None, "slab", None, None), P(), P(band), P(band, "slab", None)),
        out_specs=(P(band, "slab", None), P(band, "slab", None)),
        check_vma=False,
    )
```

```python
import math

import jax
import jax.numpy as jnp
from jax import lax
from jax.sharding import Mesh, PartitionSpec as P

grid_spacing = 0.59
wigner_a = 0.44
wigner_b = 7.8


def dft_tables(extent):
    indices = jnp.arange(extent, dtype=jnp.int32)
    phase = indices[:, None] * indices[None, :] % extent
    angle = phase.astype(jnp.float32) * (2.0 * math.pi / extent)
    return (jnp.cos(angle), jnp.sin(angle))


def kernel_block(extent, starts, amounts):
    pieces = []
    for offset, amount in zip(starts, amounts):
        frequency = offset + jnp.arange(amount, dtype=jnp.int32)
        shifted = (frequency + extent // 2) % extent - extent // 2
        pieces.append(shifted * shifted)
    squared = pieces[0][:, None, None] + pieces[1][None, :, None] + pieces[2][None, None, :]
    length = extent * grid_spacing
    scaled = length * length / math.pi / jnp.maximum(squared, 1).astype(jnp.float32)
    return jnp.where(squared == 0, 0.0, scaled)


def exchange_correlation(density):
    root_density = jnp.cbrt(density)
    radius = (3.0 / (4.0 * math.pi)) ** (1.0 / 3.0) / root_density
    exchange_part = -((3.0 / math.pi) ** (1.0 / 3.0)) * root_density
    shifted = radius + wigner_b
    correlation = -wigner_a / shifted - wigner_a * radius / (3.0 * shifted * shifted)
    return exchange_part + correlation


def project(pattern, values, matrix, precision=lax.Precision.HIGHEST):
    return jnp.einsum(pattern, values, matrix, precision=precision)


def rotate(real_part, imag_part, pattern, cosine_table, sine_table, direction):
    fast = lax.Precision.HIGH
    new_real = project(pattern, real_part, cosine_table, fast) - direction * project(
        pattern, imag_part, sine_table, fast
    )
    new_imag = direction * project(pattern, real_part, sine_table, fast) + project(
        pattern, imag_part, cosine_table, fast
    )
    return (new_real, new_imag)


def real_basis(extent):
    half = extent // 2
    indices = jnp.arange(extent, dtype=jnp.int32)
    frequency = jnp.where(indices <= half, indices, indices - half)
    phase = frequency[:, None] * indices[None, :] % extent
    angle = phase.astype(jnp.float32) * (2.0 * math.pi / extent)
    basis = jnp.where((indices <= half)[:, None], jnp.cos(angle), jnp.sin(angle))
    weight = jnp.where((indices == 0) | (indices == half), 1.0, 2.0).astype(jnp.float32)
    return basis, frequency, weight


def real_kernel_block(extent, frequency, weight, start, amount):
    rows = lax.dynamic_slice_in_dim(frequency, start, amount, 0)
    row_weight = lax.dynamic_slice_in_dim(weight, start, amount, 0)
    squared = (
        (rows * rows)[:, None, None]
        + (frequency * frequency)[None, :, None]
        + (frequency * frequency)[None, None, :]
    )
    length = extent * grid_spacing
    scaled = length * length / math.pi / jnp.maximum(squared, 1).astype(jnp.float32)
    kernel = jnp.where(squared == 0, 0.0, scaled)
    scale = row_weight[:, None, None] * weight[None, :, None] * weight[None, None, :]
    return kernel * scale / float(extent) ** 3


def support(values, axis, radius):
    extent = values.shape[axis]
    low = lax.slice_in_dim(values, 0, radius + 1, axis=axis)
    high = lax.slice_in_dim(values, extent - radius, extent, axis=axis)
    return jnp.concatenate((low, high), axis=axis)


def keep_slabs(values, live):
    runs = []
    for slab in live:
        if runs and runs[-1][1] == slab:
            runs[-1][1] = slab + 1
        else:
            runs.append([slab, slab + 1])
    pieces = [values[start:stop] for start, stop in runs]
    return pieces[0] if len(pieces) == 1 else jnp.concatenate(pieces, axis=0)


def exchange(values, axis_name, split_axis, concat_axis):
    count = lax.axis_size(axis_name)
    shape = values.shape
    chunk = shape[split_axis] // count
    parts = values.reshape(shape[:split_axis] + (count, chunk) + shape[split_axis + 1 :])
    parts = jnp.moveaxis(parts, split_axis, 0)
    inner = parts.shape[1:]
    parts = lax.all_to_all(parts.reshape(count, -1), axis_name, 0, 0, tiled=True)
    parts = jnp.moveaxis(parts.reshape((count,) + inner), 0, concat_axis)
    merged = list(inner)
    merged[concat_axis] *= count
    return parts.reshape(merged)


def block_kernel(extent, frequency, weight, first, second):
    rows_a = lax.dynamic_slice_in_dim(frequency, first[0], first[1], 0)
    rows_b = lax.dynamic_slice_in_dim(frequency, second[0], second[1], 0)
    weight_a = lax.dynamic_slice_in_dim(weight, first[0], first[1], 0)
    weight_b = lax.dynamic_slice_in_dim(weight, second[0], second[1], 0)
    squared = (
        (frequency * frequency)[:, None, None]
        + (rows_a * rows_a)[None, :, None]
        + (rows_b * rows_b)[None, None, :]
    )
    length = extent * grid_spacing
    scaled = length * length / math.pi / jnp.maximum(squared, 1).astype(jnp.float32)
    kernel = jnp.where(squared == 0, 0.0, scaled)
    scale = weight[:, None, None] * weight_a[None, :, None] * weight_b[None, None, :]
    return kernel * scale / float(extent) ** 3


def local(wave_coeffs, column_mask, occupations, core_density):
    local_bands = wave_coeffs.shape[0]
    row_count = wave_coeffs.shape[2]
    extent = wave_coeffs.shape[3]
    plane_count = lax.axis_size("plane")
    half_count = lax.axis_size("half")
    band_count = plane_count * half_count
    bands_all = band_count * local_bands
    band_rows = extent // band_count
    slab_count = lax.axis_size("slab")
    slab_index = lax.axis_index("slab")
    radius = extent // 4
    cosine_table, sine_table = dft_tables(extent)
    cosine_kept = support(cosine_table, 0, radius)
    sine_kept = support(sine_table, 0, radius)
    mask_rows = lax.dynamic_slice_in_dim(column_mask, slab_index * row_count, row_count, 0)
    mask_kept = support(mask_rows, 1, radius).astype(jnp.float32)
    masked = support(wave_coeffs, 3, radius) * mask_kept[None, None, :, :, None]
    live = [
        slab
        for slab in range(slab_count)
        if any(
            abs((row + extent // 2) % extent - extent // 2) <= extent // 4
            for row in range(slab * row_count, (slab + 1) * row_count)
        )
    ]
    blocked_cosine = keep_slabs(cosine_table.reshape(slab_count, row_count, extent), live)
    blocked_sine = keep_slabs(sine_table.reshape(slab_count, row_count, extent), live)
    factor = 1.0 / (float(extent) ** 3 * bands_all)
    weights = occupations * factor
    partial_value = None
    for member in range(local_bands):
        real_part, imag_part = rotate(
            masked[member, 0], masked[member, 1], "xyz,zw->wxy", cosine_table, sine_table, 1.0
        )
        stacked = jnp.stack((real_part, imag_part), axis=1).reshape(slab_count, -1)
        arrived = lax.all_to_all(stacked, "slab", split_axis=0, concat_axis=0, tiled=True)
        arrived = keep_slabs(
            arrived.reshape(slab_count, extent // slab_count, 2, row_count, 2 * radius + 1), live
        )
        real_part, imag_part = rotate(
            arrived[:, :, 0], arrived[:, :, 1], "szgy,sgw->zwy", blocked_cosine, blocked_sine, 1.0
        )
        plane_real, plane_imag = rotate(
            real_part, imag_part, "zxy,yw->zxw", cosine_kept, sine_kept, 1.0
        )
        term = weights[member] * (plane_real * plane_real + plane_imag * plane_imag)
        partial_value = term if partial_value is None else partial_value + term
    basis, frequency, weight = real_basis(extent)
    plane_rows = half_count * band_rows
    spread = partial_value.reshape(row_count, plane_count, plane_rows, extent)
    density = lax.all_to_all(spread, "plane", split_axis=1, concat_axis=1, tiled=True).sum(axis=1)
    spectrum = project("zxy,my->zxm", density, basis)
    spectrum = exchange(spectrum, "plane", 2, 1)
    spectrum = project("zxm,nx->znm", spectrum, basis)
    spectrum = exchange(spectrum, "slab", 1, 0)
    spectrum = project("zab,mz->mab", spectrum, basis)
    plane_index = lax.axis_index("plane")
    kernel = block_kernel(
        extent,
        frequency,
        weight,
        (slab_index * row_count, row_count),
        (plane_index * (extent // plane_count), extent // plane_count),
    )
    potential = project("mab,mz->zab", kernel * spectrum, basis)
    potential = exchange(potential, "slab", 0, 1)
    potential = project("znm,nx->zxm", potential, basis)
    potential = exchange(potential, "plane", 1, 2)
    potential = project("zxm,my->zxy", potential, basis)
    summed = jnp.stack((density, potential))
    summed = summed.reshape(2, row_count, half_count, band_rows, slab_count, row_count)
    summed = jnp.transpose(summed, (2, 4, 0, 1, 3, 5)).reshape(
        half_count * slab_count, 2, row_count, band_rows, row_count
    )
    arrived = lax.all_to_all(summed, ("half", "slab"), split_axis=0, concat_axis=0, tiled=True)
    arrived = arrived.reshape(half_count, slab_count, 2, row_count, band_rows, row_count).sum(axis=0)
    placed = jnp.transpose(arrived, (1, 3, 4, 0, 2)).reshape(2, band_rows, row_count, extent)
    own_density, hartree = placed[0], placed[1]
    xc_potential = exchange_correlation(own_density + core_density)
    return (hartree, xc_potential)


def solution(mesh):
    band_count, slab_count = mesh.devices.shape
    split_mesh = Mesh(
        mesh.devices.reshape(band_count // 2, 2, slab_count), ("plane", "half", "slab")
    )
    band = ("plane", "half")
    return jax.shard_map(
        local,
        mesh=split_mesh,
        in_specs=(P(band, None, "slab", None, None), P(), P(band), P(band, "slab", None)),
        out_specs=(P(band, "slab", None), P(band, "slab", None)),
        check_vma=False,
    )
```

```python
import math

import jax
import jax.numpy as jnp
from jax import lax
from jax.sharding import Mesh, PartitionSpec as P

grid_spacing = 0.59
wigner_a = 0.44
wigner_b = 7.8


def dft_tables(extent):
    indices = jnp.arange(extent, dtype=jnp.int32)
    phase = indices[:, None] * indices[None, :] % extent
    angle = phase.astype(jnp.float32) * (2.0 * math.pi / extent)
    return (jnp.cos(angle), jnp.sin(angle))


def kernel_block(extent, starts, amounts):
    pieces = []
    for offset, amount in zip(starts, amounts):
        frequency = offset + jnp.arange(amount, dtype=jnp.int32)
        shifted = (frequency + extent // 2) % extent - extent // 2
        pieces.append(shifted * shifted)
    squared = pieces[0][:, None, None] + pieces[1][None, :, None] + pieces[2][None, None, :]
    length = extent * grid_spacing
    scaled = length * length / math.pi / jnp.maximum(squared, 1).astype(jnp.float32)
    return jnp.where(squared == 0, 0.0, scaled)


def exchange_correlation(density):
    root_density = jnp.cbrt(density)
    radius = (3.0 / (4.0 * math.pi)) ** (1.0 / 3.0) / root_density
    exchange_part = -((3.0 / math.pi) ** (1.0 / 3.0)) * root_density
    shifted = radius + wigner_b
    correlation = -wigner_a / shifted - wigner_a * radius / (3.0 * shifted * shifted)
    return exchange_part + correlation


def project(pattern, values, matrix, precision=lax.Precision.HIGHEST):
    return jnp.einsum(pattern, values, matrix, precision=precision)


def rotate(real_part, imag_part, pattern, cosine_table, sine_table, direction):
    fast = lax.Precision.HIGH
    new_real = project(pattern, real_part, cosine_table, fast) - direction * project(
        pattern, imag_part, sine_table, fast
    )
    new_imag = direction * project(pattern, real_part, sine_table, fast) + project(
        pattern, imag_part, cosine_table, fast
    )
    return (new_real, new_imag)


def real_basis(extent):
    half = extent // 2
    indices = jnp.arange(extent, dtype=jnp.int32)
    frequency = jnp.where(indices <= half, indices, indices - half)
    phase = frequency[:, None] * indices[None, :] % extent
    angle = phase.astype(jnp.float32) * (2.0 * math.pi / extent)
    basis = jnp.where((indices <= half)[:, None], jnp.cos(angle), jnp.sin(angle))
    weight = jnp.where((indices == 0) | (indices == half), 1.0, 2.0).astype(jnp.float32)
    return basis, frequency, weight


def real_kernel_block(extent, frequency, weight, start, amount):
    rows = lax.dynamic_slice_in_dim(frequency, start, amount, 0)
    row_weight = lax.dynamic_slice_in_dim(weight, start, amount, 0)
    squared = (
        (rows * rows)[:, None, None]
        + (frequency * frequency)[None, :, None]
        + (frequency * frequency)[None, None, :]
    )
    length = extent * grid_spacing
    scaled = length * length / math.pi / jnp.maximum(squared, 1).astype(jnp.float32)
    kernel = jnp.where(squared == 0, 0.0, scaled)
    scale = row_weight[:, None, None] * weight[None, :, None] * weight[None, None, :]
    return kernel * scale / float(extent) ** 3


def support(values, axis, radius):
    extent = values.shape[axis]
    low = lax.slice_in_dim(values, 0, radius + 1, axis=axis)
    high = lax.slice_in_dim(values, extent - radius, extent, axis=axis)
    return jnp.concatenate((low, high), axis=axis)


def keep_slabs(values, live):
    runs = []
    for slab in live:
        if runs and runs[-1][1] == slab:
            runs[-1][1] = slab + 1
        else:
            runs.append([slab, slab + 1])
    pieces = [values[start:stop] for start, stop in runs]
    return pieces[0] if len(pieces) == 1 else jnp.concatenate(pieces, axis=0)


def exchange(values, axis_name, split_axis, concat_axis):
    count = lax.axis_size(axis_name)
    shape = values.shape
    chunk = shape[split_axis] // count
    parts = values.reshape(shape[:split_axis] + (count, chunk) + shape[split_axis + 1 :])
    parts = jnp.moveaxis(parts, split_axis, 0)
    inner = parts.shape[1:]
    parts = lax.all_to_all(parts.reshape(count, -1), axis_name, 0, 0, tiled=True)
    parts = jnp.moveaxis(parts.reshape((count,) + inner), 0, concat_axis)
    merged = list(inner)
    merged[concat_axis] *= count
    return parts.reshape(merged)


def block_kernel(extent, frequency, weight, first, second):
    rows_a = lax.dynamic_slice_in_dim(frequency, first[0], first[1], 0)
    rows_b = lax.dynamic_slice_in_dim(frequency, second[0], second[1], 0)
    weight_a = lax.dynamic_slice_in_dim(weight, first[0], first[1], 0)
    weight_b = lax.dynamic_slice_in_dim(weight, second[0], second[1], 0)
    squared = (
        (frequency * frequency)[:, None, None]
        + (rows_a * rows_a)[None, :, None]
        + (rows_b * rows_b)[None, None, :]
    )
    length = extent * grid_spacing
    scaled = length * length / math.pi / jnp.maximum(squared, 1).astype(jnp.float32)
    kernel = jnp.where(squared == 0, 0.0, scaled)
    scale = weight[:, None, None] * weight_a[None, :, None] * weight_b[None, None, :]
    return kernel * scale / float(extent) ** 3


def local(wave_coeffs, column_mask, occupations, core_density):
    local_bands = wave_coeffs.shape[0]
    row_count = wave_coeffs.shape[2]
    extent = wave_coeffs.shape[3]
    plane_count = lax.axis_size("plane")
    half_count = lax.axis_size("half")
    band_count = plane_count * half_count
    bands_all = band_count * local_bands
    band_rows = extent // band_count
    slab_count = lax.axis_size("slab")
    slab_index = lax.axis_index("slab")
    radius = extent // 4
    cosine_table, sine_table = dft_tables(extent)
    cosine_kept = support(cosine_table, 0, radius)
    sine_kept = support(sine_table, 0, radius)
    mask_rows = lax.dynamic_slice_in_dim(column_mask, slab_index * row_count, row_count, 0)
    mask_kept = support(mask_rows, 1, radius).astype(jnp.float32)
    masked = support(wave_coeffs, 3, radius) * mask_kept[None, None, :, :, None]
    real_part, imag_part = rotate(
        masked[:, 0], masked[:, 1], "bxyz,zw->wbxy", cosine_table, sine_table, 1.0
    )
    stacked = jnp.stack((real_part, imag_part), axis=2).reshape(slab_count, -1)
    arrived = lax.all_to_all(stacked, "slab", split_axis=0, concat_axis=0, tiled=True)
    arrived = arrived.reshape(
        slab_count, extent // slab_count, local_bands, 2, row_count, 2 * radius + 1
    )
    blocked_cosine = cosine_table.reshape(slab_count, row_count, extent)
    blocked_sine = sine_table.reshape(slab_count, row_count, extent)
    live = [
        slab
        for slab in range(slab_count)
        if any(
            abs((row + extent // 2) % extent - extent // 2) <= extent // 4
            for row in range(slab * row_count, (slab + 1) * row_count)
        )
    ]
    arrived = keep_slabs(arrived, live)
    blocked_cosine = keep_slabs(blocked_cosine, live)
    blocked_sine = keep_slabs(blocked_sine, live)
    real_part, imag_part = rotate(
        arrived[:, :, :, 0], arrived[:, :, :, 1], "szbgy,sgw->bzwy", blocked_cosine, blocked_sine, 1.0
    )
    plane_real, plane_imag = rotate(
        real_part, imag_part, "bzxy,yw->bzxw", cosine_kept, sine_kept, 1.0
    )
    factor = 1.0 / (float(extent) ** 3 * bands_all)
    weights = occupations * factor
    modulus = plane_real * plane_real + plane_imag * plane_imag
    partial_value = weights[0] * modulus[0]
    for member in range(1, local_bands):
        partial_value = partial_value + weights[member] * modulus[member]
    basis, frequency, weight = real_basis(extent)
    plane_rows = half_count * band_rows
    spread = partial_value.reshape(row_count, plane_count, plane_rows, extent)
    density = lax.all_to_all(spread, "plane", split_axis=1, concat_axis=1, tiled=True).sum(axis=1)
    spectrum = project("zxy,my->zxm", density, basis)
    spectrum = exchange(spectrum, "plane", 2, 1)
    spectrum = project("zxm,nx->znm", spectrum, basis)
    spectrum = exchange(spectrum, "slab", 1, 0)
    spectrum = project("zab,mz->mab", spectrum, basis)
    plane_index = lax.axis_index("plane")
    kernel = block_kernel(
        extent,
        frequency,
        weight,
        (slab_index * row_count, row_count),
        (plane_index * (extent // plane_count), extent // plane_count),
    )
    potential = project("mab,mz->zab", kernel * spectrum, basis, lax.Precision.HIGH)
    potential = exchange(potential, "slab", 0, 1)
    potential = project("znm,nx->zxm", potential, basis, lax.Precision.HIGH)
    potential = exchange(potential, "plane", 1, 2)
    potential = project("zxm,my->zxy", potential, basis, lax.Precision.HIGH)
    summed = jnp.stack((density, potential))
    summed = summed.reshape(2, row_count, half_count, band_rows, slab_count, row_count)
    summed = jnp.transpose(summed, (2, 4, 0, 1, 3, 5)).reshape(
        half_count * slab_count, 2, row_count, band_rows, row_count
    )
    arrived = lax.all_to_all(summed, ("half", "slab"), split_axis=0, concat_axis=0, tiled=True)
    arrived = arrived.reshape(half_count, slab_count, 2, row_count, band_rows, row_count).sum(axis=0)
    placed = jnp.transpose(arrived, (1, 3, 4, 0, 2)).reshape(2, band_rows, row_count, extent)
    own_density, hartree = placed[0], placed[1]
    xc_potential = exchange_correlation(own_density + core_density)
    return (hartree, xc_potential)


def solution(mesh):
    band_count, slab_count = mesh.devices.shape
    split_mesh = Mesh(
        mesh.devices.reshape(band_count // 2, 2, slab_count), ("plane", "half", "slab")
    )
    band = ("plane", "half")
    return jax.shard_map(
        local,
        mesh=split_mesh,
        in_specs=(P(band, None, "slab", None, None), P(), P(band), P(band, "slab", None)),
        out_specs=(P(band, "slab", None), P(band, "slab", None)),
        check_vma=False,
    )
```

```python
import math

import jax
import jax.numpy as jnp
from jax import lax
from jax.sharding import Mesh, PartitionSpec as P

grid_spacing = 0.59
wigner_a = 0.44
wigner_b = 7.8


def dft_tables(extent):
    indices = jnp.arange(extent, dtype=jnp.int32)
    phase = indices[:, None] * indices[None, :] % extent
    angle = phase.astype(jnp.float32) * (2.0 * math.pi / extent)
    return (jnp.cos(angle), jnp.sin(angle))


def kernel_block(extent, starts, amounts):
    pieces = []
    for offset, amount in zip(starts, amounts):
        frequency = offset + jnp.arange(amount, dtype=jnp.int32)
        shifted = (frequency + extent // 2) % extent - extent // 2
        pieces.append(shifted * shifted)
    squared = pieces[0][:, None, None] + pieces[1][None, :, None] + pieces[2][None, None, :]
    length = extent * grid_spacing
    scaled = length * length / math.pi / jnp.maximum(squared, 1).astype(jnp.float32)
    return jnp.where(squared == 0, 0.0, scaled)


def exchange_correlation(density):
    root_density = jnp.cbrt(density)
    radius = (3.0 / (4.0 * math.pi)) ** (1.0 / 3.0) / root_density
    exchange_part = -((3.0 / math.pi) ** (1.0 / 3.0)) * root_density
    shifted = radius + wigner_b
    correlation = -wigner_a / shifted - wigner_a * radius / (3.0 * shifted * shifted)
    return exchange_part + correlation


def project(pattern, values, matrix, precision=lax.Precision.HIGHEST):
    return jnp.einsum(pattern, values, matrix, precision=precision)


def rotate(real_part, imag_part, pattern, cosine_table, sine_table, direction):
    fast = lax.Precision.HIGH
    new_real = project(pattern, real_part, cosine_table, fast) - direction * project(
        pattern, imag_part, sine_table, fast
    )
    new_imag = direction * project(pattern, real_part, sine_table, fast) + project(
        pattern, imag_part, cosine_table, fast
    )
    return (new_real, new_imag)


def real_basis(extent):
    half = extent // 2
    indices = jnp.arange(extent, dtype=jnp.int32)
    frequency = jnp.where(indices <= half, indices, indices - half)
    phase = frequency[:, None] * indices[None, :] % extent
    angle = phase.astype(jnp.float32) * (2.0 * math.pi / extent)
    basis = jnp.where((indices <= half)[:, None], jnp.cos(angle), jnp.sin(angle))
    weight = jnp.where((indices == 0) | (indices == half), 1.0, 2.0).astype(jnp.float32)
    return basis, frequency, weight


def real_kernel_block(extent, frequency, weight, start, amount):
    rows = lax.dynamic_slice_in_dim(frequency, start, amount, 0)
    row_weight = lax.dynamic_slice_in_dim(weight, start, amount, 0)
    squared = (
        (rows * rows)[:, None, None]
        + (frequency * frequency)[None, :, None]
        + (frequency * frequency)[None, None, :]
    )
    length = extent * grid_spacing
    scaled = length * length / math.pi / jnp.maximum(squared, 1).astype(jnp.float32)
    kernel = jnp.where(squared == 0, 0.0, scaled)
    scale = row_weight[:, None, None] * weight[None, :, None] * weight[None, None, :]
    return kernel * scale / float(extent) ** 3


def support(values, axis, radius):
    extent = values.shape[axis]
    low = lax.slice_in_dim(values, 0, radius + 1, axis=axis)
    high = lax.slice_in_dim(values, extent - radius, extent, axis=axis)
    return jnp.concatenate((low, high), axis=axis)


def keep_slabs(values, live):
    runs = []
    for slab in live:
        if runs and runs[-1][1] == slab:
            runs[-1][1] = slab + 1
        else:
            runs.append([slab, slab + 1])
    pieces = [values[start:stop] for start, stop in runs]
    return pieces[0] if len(pieces) == 1 else jnp.concatenate(pieces, axis=0)


def exchange(values, axis_name, split_axis, concat_axis):
    count = lax.axis_size(axis_name)
    shape = values.shape
    chunk = shape[split_axis] // count
    parts = values.reshape(shape[:split_axis] + (count, chunk) + shape[split_axis + 1 :])
    parts = jnp.moveaxis(parts, split_axis, 0)
    inner = parts.shape[1:]
    parts = lax.all_to_all(parts.reshape(count, -1), axis_name, 0, 0, tiled=True)
    parts = jnp.moveaxis(parts.reshape((count,) + inner), 0, concat_axis)
    merged = list(inner)
    merged[concat_axis] *= count
    return parts.reshape(merged)


def block_kernel(extent, frequency, weight, first, second):
    rows_a = lax.dynamic_slice_in_dim(frequency, first[0], first[1], 0)
    rows_b = lax.dynamic_slice_in_dim(frequency, second[0], second[1], 0)
    weight_a = lax.dynamic_slice_in_dim(weight, first[0], first[1], 0)
    weight_b = lax.dynamic_slice_in_dim(weight, second[0], second[1], 0)
    squared = (
        (frequency * frequency)[:, None, None]
        + (rows_a * rows_a)[None, :, None]
        + (rows_b * rows_b)[None, None, :]
    )
    length = extent * grid_spacing
    scaled = length * length / math.pi / jnp.maximum(squared, 1).astype(jnp.float32)
    kernel = jnp.where(squared == 0, 0.0, scaled)
    scale = weight[:, None, None] * weight_a[None, :, None] * weight_b[None, None, :]
    return kernel * scale / float(extent) ** 3


def local(wave_coeffs, column_mask, occupations, core_density):
    local_bands = wave_coeffs.shape[0]
    row_count = wave_coeffs.shape[2]
    extent = wave_coeffs.shape[3]
    plane_count = lax.axis_size("plane")
    half_count = lax.axis_size("half")
    band_count = plane_count * half_count
    bands_all = band_count * local_bands
    band_rows = extent // band_count
    slab_count = lax.axis_size("slab")
    slab_index = lax.axis_index("slab")
    radius = extent // 4
    cosine_table, sine_table = dft_tables(extent)
    cosine_kept = support(cosine_table, 0, radius)
    sine_kept = support(sine_table, 0, radius)
    mask_rows = lax.dynamic_slice_in_dim(column_mask, slab_index * row_count, row_count, 0)
    mask_kept = support(mask_rows, 1, radius).astype(jnp.float32)
    masked = support(wave_coeffs, 3, radius) * mask_kept[None, None, :, :, None]
    real_part, imag_part = rotate(
        masked[:, 0], masked[:, 1], "bxyz,zw->wbxy", cosine_table, sine_table, 1.0
    )
    stacked = jnp.stack((real_part, imag_part), axis=2).reshape(slab_count, -1)
    arrived = lax.all_to_all(stacked, "slab", split_axis=0, concat_axis=0, tiled=True)
    arrived = arrived.reshape(
        slab_count, extent // slab_count, local_bands, 2, row_count, 2 * radius + 1
    )
    blocked_cosine = cosine_table.reshape(slab_count, row_count, extent)
    blocked_sine = sine_table.reshape(slab_count, row_count, extent)
    live = [
        slab
        for slab in range(slab_count)
        if any(
            abs((row + extent // 2) % extent - extent // 2) <= extent // 4
            for row in range(slab * row_count, (slab + 1) * row_count)
        )
    ]
    arrived = keep_slabs(arrived, live)
    blocked_cosine = keep_slabs(blocked_cosine, live)
    blocked_sine = keep_slabs(blocked_sine, live)
    real_part, imag_part = rotate(
        arrived[:, :, :, 0], arrived[:, :, :, 1], "szbgy,sgw->bzwy", blocked_cosine, blocked_sine, 1.0
    )
    plane_real, plane_imag = rotate(
        real_part, imag_part, "bzxy,yw->bzxw", cosine_kept, sine_kept, 1.0
    )
    factor = 1.0 / (float(extent) ** 3 * bands_all)
    weights = occupations * factor
    modulus = plane_real * plane_real + plane_imag * plane_imag
    partial_value = weights[0] * modulus[0]
    for member in range(1, local_bands):
        partial_value = partial_value + weights[member] * modulus[member]
    basis, frequency, weight = real_basis(extent)
    plane_rows = half_count * band_rows
    spread = partial_value.reshape(row_count, plane_count, plane_rows, extent)
    density = lax.all_to_all(spread, "plane", split_axis=1, concat_axis=1, tiled=True).sum(axis=1)
    spectrum = project("zxy,my->zxm", density, basis)
    spectrum = exchange(spectrum, "plane", 2, 1)
    spectrum = project("zxm,nx->znm", spectrum, basis)
    spectrum = exchange(spectrum, "slab", 1, 0)
    spectrum = project("zab,mz->mab", spectrum, basis)
    plane_index = lax.axis_index("plane")
    kernel = block_kernel(
        extent,
        frequency,
        weight,
        (slab_index * row_count, row_count),
        (plane_index * (extent // plane_count), extent // plane_count),
    )
    potential = project("mab,mz->zab", kernel * spectrum, basis, lax.Precision.HIGH)
    potential = exchange(potential, "slab", 0, 1)
    potential = project("znm,nx->zxm", potential, basis, lax.Precision.HIGH)
    potential = exchange(potential, "plane", 1, 2)
    potential = project("zxm,my->zxy", potential, basis, lax.Precision.HIGH)
    summed = jnp.stack((density, potential))
    summed = summed.reshape(2, row_count, half_count, band_rows, slab_count, row_count)
    summed = jnp.transpose(summed, (2, 4, 0, 1, 3, 5)).reshape(
        half_count * slab_count, 2, row_count, band_rows, row_count
    )
    arrived = lax.all_to_all(summed, ("half", "slab"), split_axis=0, concat_axis=0, tiled=True)
    arrived = arrived.reshape(half_count, slab_count, 2, row_count, band_rows, row_count)

    def place(which):
        total = arrived[:, :, which].sum(axis=0)
        return jnp.transpose(total, (2, 3, 0, 1)).reshape(band_rows, row_count, extent)

    hartree = place(1)
    xc_potential = exchange_correlation(place(0) + core_density)
    return (hartree, xc_potential)


def solution(mesh):
    band_count, slab_count = mesh.devices.shape
    split_mesh = Mesh(
        mesh.devices.reshape(band_count // 2, 2, slab_count), ("plane", "half", "slab")
    )
    band = ("plane", "half")
    return jax.shard_map(
        local,
        mesh=split_mesh,
        in_specs=(P(band, None, "slab", None, None), P(), P(band), P(band, "slab", None)),
        out_specs=(P(band, "slab", None), P(band, "slab", None)),
        check_vma=False,
    )
```
